128 devices in a mesh: row: 8 (over z, core), col: 16 (over x, y).
Axes of the slice: x: 4, y: 4, z: 4, core: 2. Of those that a mesh axis runs over, the one named last changes fastest.
Arguments:
- logarithmic_conductivity: float32 [64, 512, 2048], P(None, 'row', 'col'), may hold values from -0.6 to 0.6
- starting_head: bfloat16 [64, 512, 2048], P(None, 'row', 'col'), may hold values from -4 to 4
- recharge: float32 [512, 2048], P('row', 'col'), may hold values from -4 to 4
- well_cells: int32 [4, 256], replicated, may hold values from 0 to 8191
- well_owner: int32 [4], replicated, may hold values from 0 to 127
- observed: float32 [1024], replicated, may hold values from -4 to 4
- obs_var: float32 [1024], replicated, may hold values from 0.25 to 4
- perturb: float32 [64, 1024], replicated, may hold values from -4 to 4
Outputs:
- pressure_out: bfloat16 [64, 512, 2048], P(None, 'row', 'col')
- predicted: float32 [64, 1024], replicated
- updated_perm: float32 [64, 512, 2048], P(None, 'row', 'col')
The draws below stay inside these ranges and needn't reach their ends.
Inputs may be any that keep to these rules, and one draw needn't show every extreme that they name: Well k of group g is the cell well_cells[g, k] (row-major) of the tile of device well_owner[g]; wells may repeat. `well_owner`: devices are numbered row index * the size of col + col index; groups may share an owner.
All inputs are finite; a program needn't handle non-finite values.
Results may differ from the reference program's by a relative error of at most 0.001.
Values sent between devices are 32-bit elements; how exact they have to be, the bound alone decides.
No kernel may reach another device: no remote copies, remote signals or barrier semaphores. Data moves between devices by JAX's collectives and lax.ppermute only.
A program may use at most 128 MiB of HBM per device.

```python
import math
import jax
import jax.numpy as jnp
from jax import lax

REALIZATIONS = 64
ROWS_DEV = 64
COLS_DEV = 128
STEPS = 3
GROUPS = 4
WELLS = 256
ND = 1024
NX = 512
NY = 2048
N_COL = 16
DEVICES = 128


def place_ends(result, own_key, least, top_value):
    place = [jax.random.randint(jax.random.fold_in(own_key, axis), (), 0, length) for axis, length in enumerate(result.shape)]
    main_axis = result.shape.index(max(result.shape))
    next_to = place[:main_axis] + [(place[main_axis] + 1) % result.shape[main_axis]] + place[main_axis + 1:]
    return result.at[tuple(place)].set(least).at[tuple(next_to)].set(top_value)


def shard_levels(own_key, extent, cuts, least, top_value):
    loudness = 1.0
    for dim, shards_of in cuts:
        heights = jax.random.uniform(jax.random.fold_in(jax.random.fold_in(own_key, 6), dim), (shards_of,), jnp.float32, least / len(cuts), top_value / len(cuts))
        loudness = loudness * jnp.repeat(jnp.exp(heights), extent[dim] // shards_of).reshape((-1,) + (1,) * (len(extent) - 1 - dim))
    return loudness


def normal_values(rng, extent, scale, limit, split=(), kind=jnp.bfloat16):
    entries = jax.random.normal(rng, extent, jnp.float32) * scale
    if len(split) > 0:
        entries = shard_levels(rng, extent, split, -0.22, 0.18) * entries
    return jnp.clip(entries, min=-limit, max=limit).astype(kind)


def setup_inputs(seed: int = 0) -> dict:
    key_list = jax.random.split(jax.random.key(seed), 9)
    logarithmic_conductivity = jnp.clip(jax.random.uniform(key_list[0], (REALIZATIONS, NX, NY), jnp.float32, -0.6, 0.6) * shard_levels(key_list[0], (REALIZATIONS, NX, NY), ((1, 8), (2, 16)), -0.4, 0.0), -0.6, 0.6)
    starting_head = normal_values(key_list[1], (REALIZATIONS, NX, NY), 1.0, 4.0, ((1, 8), (2, 16)))
    recharge = normal_values(key_list[2], (NX, NY), 1.0, 4.0, ((0, 8), (1, 16)), jnp.float32)
    well_cells = place_ends(jax.random.randint(key_list[3], (GROUPS, WELLS), 0, ROWS_DEV * COLS_DEV), jax.random.fold_in(key_list[3], 1), 0, (ROWS_DEV * COLS_DEV) - 1).astype(jnp.int32)
    well_owner = place_ends(jax.random.randint(key_list[4], (GROUPS,), 0, DEVICES), jax.random.fold_in(key_list[4], 1), 0, DEVICES - 1).astype(jnp.int32)
    observed = normal_values(key_list[5], (ND,), 1.0, 4.0, (), jnp.float32)
    obs_var = jnp.clip(jnp.exp(jax.random.uniform(key_list[6], (ND,), jnp.float32, math.log(0.25), math.log(4.0))), 0.25, 4.0)
    perturb = normal_values(key_list[7], (REALIZATIONS, ND), 1.0, 4.0, (), jnp.float32)
    return dict(logarithmic_conductivity=logarithmic_conductivity, starting_head=starting_head, recharge=recharge, well_cells=well_cells, well_owner=well_owner, observed=observed, obs_var=obs_var, perturb=perturb)


time_step = 0.13

def neighbours(padded):
    return (padded[:, :-2, 1:-1], padded[:, 2:, 1:-1], padded[:, 1:-1, :-2], padded[:, 1:-1, 2:])

def advance(padded_perm, bordered_head, source):
    centre_perm = padded_perm[:, 1:-1, 1:-1]
    centre_press = bordered_head[:, 1:-1, 1:-1]
    flux_total = jnp.zeros_like(centre_press)
    for near_perm, near_press in zip(neighbours(padded_perm), neighbours(bordered_head)):
        flux_total = flux_total + jnp.exp(0.5 * (centre_perm + near_perm)) * (near_press - centre_press)
    return centre_press + time_step * (flux_total + source)

def blending_weights(predicted, observed, obs_var, perturb):
    member_count = predicted.shape[0]
    ensemble_spread = math.sqrt(member_count - 1)
    centred = (predicted - lax.optimization_barrier(jnp.mean(predicted, axis=0, keepdims=True))) / ensemble_spread
    innovation = observed[None, :] + jnp.sqrt(obs_var)[None, :] * perturb - predicted
    weighted = centred / obs_var[None, :]
    system = jnp.eye(member_count, dtype=centred.dtype) + jnp.dot(weighted, centred.T, precision=lax.Precision.HIGHEST)
    right_side = jnp.dot(weighted, innovation.T, precision=lax.Precision.HIGHEST)
    factor = jnp.linalg.cholesky(system)
    half_solved = lax.linalg.triangular_solve(factor, right_side, left_side=True, lower=True)
    return lax.linalg.triangular_solve(factor, half_solved, left_side=True, lower=True, transpose_a=True)

def reference(logarithmic_conductivity, starting_head, recharge, well_cells, well_owner, observed, obs_var, perturb):

    def predicted_readings(realization_number):
        member_perm, member_start = realization_number
        padded_perm = jnp.pad(member_perm, 1)[None]
        hydraulic_head = member_start.astype(jnp.float32)
        for step_index in range(STEPS):
            bordered_head = jnp.pad(hydraulic_head, 1)[None]
            hydraulic_head = advance(padded_perm, bordered_head, recharge[None])[0]
        return hydraulic_head
    hydraulic_head = lax.map(predicted_readings, (logarithmic_conductivity, starting_head))
    owner_row = (well_owner // N_COL).astype(jnp.int32)
    owner_col = (well_owner % N_COL).astype(jnp.int32)
    global_row = owner_row[:, None] * ROWS_DEV + well_cells // COLS_DEV
    global_col = owner_col[:, None] * COLS_DEV + well_cells % COLS_DEV
    flat_index = (global_row * NY + global_col).reshape(-1).astype(jnp.int32)
    predicted = hydraulic_head.reshape(REALIZATIONS, NX * NY)[:, flat_index]
    mixing = blending_weights(predicted, observed, obs_var, perturb)
    ensemble_spread = math.sqrt(REALIZATIONS - 1)
    anomalies = (logarithmic_conductivity - lax.optimization_barrier(jnp.mean(logarithmic_conductivity, axis=0, keepdims=True))) / ensemble_spread
    updated_perm = logarithmic_conductivity + jnp.einsum('mrc,mn->nrc', anomalies, mixing, precision=lax.Precision.HIGHEST)
    return (hydraulic_head.astype(jnp.bfloat16), predicted, updated_perm)
```

```python
import math

import jax
import jax.numpy as jnp
from jax import lax
from jax.sharding import PartitionSpec as P

STEPS = 3


time_step = 0.13


def padded_2(block, sides, width):
    for axis, dim in sides:
        count = lax.axis_size(axis)
        forward = [(i, i + 1) for i in range(count - 1)]
        backward = [(target, source) for source, target in forward]
        low = lax.ppermute(
            lax.slice_in_dim(block, block.shape[dim] - width, None, axis=dim), axis, forward
        )
        high = lax.ppermute(lax.slice_in_dim(block, 0, width, axis=dim), axis, backward)
        block = jnp.concatenate([low, block, high], axis=dim)
    return block


def butterfly(value, axis):
    count = lax.axis_size(axis)
    step = 1
    while step < count:
        value = value + lax.ppermute(value, axis, [(i, i ^ step) for i in range(count)])
        step *= 2
    return value


def neighbours(padded):
    return (padded[:, :-2, 1:-1], padded[:, 2:, 1:-1], padded[:, 1:-1, :-2], padded[:, 1:-1, 2:])


def face_terms(padded_perm):
    centre_perm = padded_perm[:, 1:-1, 1:-1]
    return [jnp.exp(0.5 * (centre_perm + near_perm)) for near_perm in neighbours(padded_perm)]


def advance(coefficients, bordered_head, source):
    centre_press = bordered_head[:, 1:-1, 1:-1]
    flux_total = jnp.zeros_like(centre_press)
    for weight_face, near_press in zip(coefficients, neighbours(bordered_head)):
        flux_total = flux_total + weight_face * (near_press - centre_press)
    return centre_press + time_step * (flux_total + source)


def blending_weights(predicted, observed, obs_var, perturb):
    member_count = predicted.shape[0]
    ensemble_spread = math.sqrt(member_count - 1)
    centred = (predicted - jnp.mean(predicted, axis=0, keepdims=True)) / ensemble_spread
    innovation = observed[None, :] + jnp.sqrt(obs_var)[None, :] * perturb - predicted
    weighted = centred / obs_var[None, :]
    system = jnp.eye(member_count, dtype=centred.dtype) + jnp.dot(
        weighted, centred.T, precision=lax.Precision.HIGHEST
    )
    right_side = jnp.dot(weighted, innovation.T, precision=lax.Precision.HIGHEST)
    factor = jnp.linalg.cholesky(system)
    half_solved = lax.linalg.triangular_solve(factor, right_side, left_side=True, lower=True)
    return lax.linalg.triangular_solve(
        factor, half_solved, left_side=True, lower=True, transpose_a=True
    )


def per_device(
    logarithmic_conductivity,
    starting_head,
    recharge,
    well_cells,
    well_owner,
    observed,
    obs_var,
    perturb,
):
    member_count, row_count, col_count = logarithmic_conductivity.shape
    initial = starting_head.astype(jnp.float32)
    padded_perm, bordered_head = (
        padded_2(logarithmic_conductivity, (("row", 1), ("col", 2)), 1),
        padded_2(initial, (("row", 1), ("col", 2)), 1),
    )
    coefficients = face_terms(padded_perm)
    hydraulic_head = advance(coefficients, bordered_head, recharge[None])
    for step_index in range(STEPS - 1):
        bordered_head = padded_2(hydraulic_head, (("row", 1), ("col", 2)), 1)
        hydraulic_head = advance(coefficients, bordered_head, recharge[None])
    flat_press = hydraulic_head.reshape(member_count, row_count * col_count)
    group_total, well_count = well_cells.shape
    local_data = jnp.take(flat_press, well_cells.reshape(-1), axis=1)
    me = lax.axis_index("row") * lax.axis_size("col") + lax.axis_index("col")
    mine = jnp.repeat(well_owner == me, well_count)
    local_data = jnp.where(mine[None, :], local_data, 0.0)
    predicted = butterfly(butterfly(local_data, "col"), "row")
    mixing = blending_weights(predicted, observed, obs_var, perturb)
    ensemble_spread = math.sqrt(member_count - 1)
    anomalies = (
        logarithmic_conductivity - jnp.mean(logarithmic_conductivity, axis=0, keepdims=True)
    ) / ensemble_spread
    updated_perm = logarithmic_conductivity + jnp.einsum(
        "mrc,mn->nrc", anomalies, mixing, precision=lax.Precision.HIGHEST
    )
    return (hydraulic_head.astype(jnp.bfloat16), predicted, updated_perm)


def solution(mesh):
    return jax.shard_map(
        per_device,
        mesh=mesh,
        in_specs=(
            P(None, "row", "col"),
            P(None, "row", "col"),
            P("row", "col"),
            P(),
            P(),
            P(),
            P(),
            P(),
        ),
        out_specs=(P(None, "row", "col"), P(), P(None, "row", "col")),
        check_vma=False,
    )
```

```python
import math

import jax
import jax.numpy as jnp
from jax import lax
from jax.sharding import PartitionSpec as P

STEPS = 3


time_step = 0.13


def exchange(block, axis, dim, width):
    count = lax.axis_size(axis)
    forward = [(i, i + 1) for i in range(count - 1)]
    backward = [(target, source) for source, target in forward]
    tail = jnp.moveaxis(lax.slice_in_dim(block, block.shape[dim] - width, None, axis=dim), dim, 0)
    head = jnp.moveaxis(lax.slice_in_dim(block, 0, width, axis=dim), dim, 0)
    low = jnp.moveaxis(lax.ppermute(tail, axis, forward), 0, dim)
    high = jnp.moveaxis(lax.ppermute(head, axis, backward), 0, dim)
    return jnp.concatenate([low, block, high], axis=dim)


def inside_grid(axis, local, width):
    first = lax.axis_index(axis) * local
    index = first + jnp.arange(-width, local + width)
    return (index >= 0) & (index < local * lax.axis_size(axis))


def butterfly(value, axis):
    count = lax.axis_size(axis)
    step = 1
    while step < count:
        value = value + lax.ppermute(value, axis, [(i, i ^ step) for i in range(count)])
        step *= 2
    return value


def neighbours(padded):
    return (padded[:, :-2, 1:-1], padded[:, 2:, 1:-1], padded[:, 1:-1, :-2], padded[:, 1:-1, 2:])


def face_terms(padded_perm):
    centre_perm = padded_perm[:, 1:-1, 1:-1]
    return [jnp.exp(0.5 * (centre_perm + near_perm)) for near_perm in neighbours(padded_perm)]


def advance(coefficients, bordered_head, source):
    centre_press = bordered_head[:, 1:-1, 1:-1]
    flux_total = jnp.zeros_like(centre_press)
    for weight_face, near_press in zip(coefficients, neighbours(bordered_head)):
        flux_total = flux_total + weight_face * (near_press - centre_press)
    return centre_press + time_step * (flux_total + source)


def blending_weights(predicted, observed, obs_var, perturb):
    member_count = predicted.shape[0]
    ensemble_spread = math.sqrt(member_count - 1)
    centred = (predicted - jnp.mean(predicted, axis=0, keepdims=True)) / ensemble_spread
    innovation = observed[None, :] + jnp.sqrt(obs_var)[None, :] * perturb - predicted
    weighted = centred / obs_var[None, :]
    system = jnp.eye(member_count, dtype=centred.dtype) + jnp.dot(
        weighted, centred.T, precision=lax.Precision.HIGHEST
    )
    right_side = jnp.dot(weighted, innovation.T, precision=lax.Precision.HIGHEST)
    factor = jnp.linalg.cholesky(system)
    half_solved = lax.linalg.triangular_solve(factor, right_side, left_side=True, lower=True)
    return lax.linalg.triangular_solve(
        factor, half_solved, left_side=True, lower=True, transpose_a=True
    )


def per_device(
    logarithmic_conductivity,
    starting_head,
    recharge,
    well_cells,
    well_owner,
    observed,
    obs_var,
    perturb,
):
    member_count, row_count, col_count = logarithmic_conductivity.shape
    width = STEPS
    stacked = jnp.concatenate(
        [logarithmic_conductivity, starting_head.astype(jnp.float32), recharge[None]], axis=0
    )
    extended = exchange(exchange(stacked, "row", 1, width), "col", 2, width)
    perm_ext = extended[:member_count]
    source_ext = extended[2 * member_count]
    hydraulic_head = extended[member_count : 2 * member_count]
    inside = inside_grid("row", row_count, width)[:, None] & inside_grid("col", col_count, width)[None, :]
    rows_ext, cols_ext = row_count + 2 * width, col_count + 2 * width
    for step_index in range(STEPS):
        lo = step_index
        perm_now = perm_ext[:, lo : rows_ext - lo, lo : cols_ext - lo]
        source_now = source_ext[lo + 1 : rows_ext - lo - 1, lo + 1 : cols_ext - lo - 1]
        hydraulic_head = advance(face_terms(perm_now), hydraulic_head, source_now[None])
        if step_index < STEPS - 1:
            keep = inside[lo + 1 : rows_ext - lo - 1, lo + 1 : cols_ext - lo - 1]
            hydraulic_head = jnp.where(keep[None], hydraulic_head, 0.0)
    flat_press = hydraulic_head.reshape(member_count, row_count * col_count)
    group_total, well_count = well_cells.shape
    local_data = jnp.take(flat_press, well_cells.reshape(-1), axis=1)
    me = lax.axis_index("row") * lax.axis_size("col") + lax.axis_index("col")
    mine = jnp.repeat(well_owner == me, well_count)
    local_data = jnp.where(mine[None, :], local_data, 0.0)
    predicted = butterfly(butterfly(local_data, "col"), "row")
    mixing = blending_weights(predicted, observed, obs_var, perturb)
    ensemble_spread = math.sqrt(member_count - 1)
    anomalies = (
        logarithmic_conductivity - jnp.mean(logarithmic_conductivity, axis=0, keepdims=True)
    ) / ensemble_spread
    updated_perm = logarithmic_conductivity + jnp.einsum(
        "mrc,mn->nrc", anomalies, mixing, precision=lax.Precision.HIGHEST
    )
    return (hydraulic_head.astype(jnp.bfloat16), predicted, updated_perm)


def solution(mesh):
    return jax.shard_map(
        per_device,
        mesh=mesh,
        in_specs=(
            P(None, "row", "col"),
            P(None, "row", "col"),
            P("row", "col"),
            P(),
            P(),
            P(),
            P(),
            P(),
        ),
        out_specs=(P(None, "row", "col"), P(), P(None, "row", "col")),
        check_vma=False,
    )
```

```python
import math

import jax
import jax.numpy as jnp
from jax import lax
from jax.sharding import PartitionSpec as P
from jax.experimental import pallas as pl
from jax.experimental.pallas import tpu as pltpu

STEPS = 3


time_step = 0.13


def send(piece, axis, forward):
    count = lax.axis_size(axis)
    pairs = [(i, i + 1) for i in range(count - 1)]
    if not forward:
        pairs = [(target, source) for source, target in pairs]
    return lax.ppermute(piece, axis, pairs)


def circular_inside(axis, local, width, size):
    index = jnp.arange(size)
    gap = (index >= local + width) & (index < size - width)
    local_index = jnp.where(index < local + width, index, index - size)
    global_index = lax.axis_index(axis) * local + local_index
    return (~gap) & (global_index >= 0) & (global_index < local * lax.axis_size(axis))


def stencil_kernel(mask_ref, source_ref, source_rows_ref, source_cols_ref, perm_ref, head_ref,
                   perm_rows_ref, head_rows_ref, perm_cols_ref, head_cols_ref, out16_ref, out32_ref):
    rows, cols = perm_ref.shape[1], perm_ref.shape[2]
    ext_rows, ext_cols = rows + 8, 2 * cols

    def extend(interior, halo_rows, halo_cols):
        return jnp.concatenate([jnp.concatenate([interior, halo_rows], axis=0), halo_cols], axis=1)

    inside = mask_ref[...] > 0.5
    source = extend(source_ref[...], source_rows_ref[0], source_cols_ref[0])

    def member(j, carry):
        perm = extend(perm_ref[j], perm_rows_ref[j], perm_cols_ref[j])
        head = extend(head_ref[j].astype(jnp.float32), head_rows_ref[j], head_cols_ref[j])
        vertical = jnp.exp(0.5 * (perm + pltpu.roll(perm, ext_rows - 1, 0)))
        horizontal = jnp.exp(0.5 * (perm + pltpu.roll(perm, ext_cols - 1, 1)))
        faces = (pltpu.roll(vertical, 1, 0), vertical, pltpu.roll(horizontal, 1, 1), horizontal)
        for _ in range(STEPS):
            near = (pltpu.roll(head, 1, 0), pltpu.roll(head, ext_rows - 1, 0),
                    pltpu.roll(head, 1, 1), pltpu.roll(head, ext_cols - 1, 1))
            flux_total = jnp.zeros_like(head)
            for weight_face, near_press in zip(faces, near):
                flux_total = flux_total + weight_face * (near_press - head)
            head = head + time_step * (flux_total + source)
            head = jnp.where(inside, head, 0.0)
        final = head[:rows, :cols]
        out32_ref[j] = final
        out16_ref[j] = final.astype(jnp.bfloat16)
        return carry

    lax.fori_loop(0, perm_ref.shape[0], member, 0)


def run_stencil(mask, source, halo_rows, halo_cols, perm, head, block):
    members, rows, cols = perm.shape
    blocks = members // block
    full2 = lambda shape: pl.BlockSpec(shape, lambda i: (0, 0))
    member_block = lambda shape, shift: pl.BlockSpec((block,) + shape, lambda i: (i + shift, 0, 0))
    last = lambda shape: pl.BlockSpec((1,) + shape, lambda i: (2 * members, 0, 0))
    ext_rows = rows + 8
    cells = members * ext_rows * 2 * cols
    return pl.pallas_call(
        stencil_kernel,
        grid=(blocks,),
        in_specs=[
            full2(mask.shape),
            full2(source.shape),
            last((8, cols)),
            last((ext_rows, cols)),
            member_block((rows, cols), 0),
            member_block((rows, cols), 0),
            member_block((8, cols), 0),
            member_block((8, cols), blocks),
            member_block((ext_rows, cols), 0),
            member_block((ext_rows, cols), blocks),
        ],
        out_specs=[member_block((rows, cols), 0), member_block((rows, cols), 0)],
        out_shape=[
            jax.ShapeDtypeStruct(perm.shape, jnp.bfloat16),
            jax.ShapeDtypeStruct(perm.shape, jnp.float32),
        ],
        cost_estimate=pl.CostEstimate(
            flops=cells * 80, transcendentals=cells * 2, bytes_accessed=members * rows * cols * 14
        ),
    )(mask, source, halo_rows, halo_cols, perm, head, halo_rows, halo_rows, halo_cols, halo_cols)


def butterfly(value, axis):
    count = lax.axis_size(axis)
    step = 1
    while step < count:
        value = value + lax.ppermute(value, axis, [(i, i ^ step) for i in range(count)])
        step *= 2
    return value


def neighbours(padded):
    return (padded[:, :-2, 1:-1], padded[:, 2:, 1:-1], padded[:, 1:-1, :-2], padded[:, 1:-1, 2:])


def face_terms(padded_perm):
    centre_perm = padded_perm[:, 1:-1, 1:-1]
    return [jnp.exp(0.5 * (centre_perm + near_perm)) for near_perm in neighbours(padded_perm)]


def advance(coefficients, bordered_head, source):
    centre_press = bordered_head[:, 1:-1, 1:-1]
    flux_total = jnp.zeros_like(centre_press)
    for weight_face, near_press in zip(coefficients, neighbours(bordered_head)):
        flux_total = flux_total + weight_face * (near_press - centre_press)
    return centre_press + time_step * (flux_total + source)


def blending_weights(predicted, observed, obs_var, perturb):
    member_count = predicted.shape[0]
    ensemble_spread = math.sqrt(member_count - 1)
    centred = (predicted - jnp.mean(predicted, axis=0, keepdims=True)) / ensemble_spread
    innovation = observed[None, :] + jnp.sqrt(obs_var)[None, :] * perturb - predicted
    weighted = centred / obs_var[None, :]
    system = jnp.eye(member_count, dtype=centred.dtype) + jnp.dot(
        weighted, centred.T, precision=lax.Precision.HIGHEST
    )
    right_side = jnp.dot(weighted, innovation.T, precision=lax.Precision.HIGHEST)
    factor = jnp.linalg.cholesky(system)
    half_solved = lax.linalg.triangular_solve(factor, right_side, left_side=True, lower=True)
    return lax.linalg.triangular_solve(
        factor, half_solved, left_side=True, lower=True, transpose_a=True
    )


def per_device(
    logarithmic_conductivity,
    starting_head,
    recharge,
    well_cells,
    well_owner,
    observed,
    obs_var,
    perturb,
):
    member_count, row_count, col_count = logarithmic_conductivity.shape
    width = STEPS
    ext_rows, ext_cols = row_count + 8, 2 * col_count
    f32 = jnp.float32

    def stack_rows(lo, hi):
        return jnp.concatenate(
            [logarithmic_conductivity[:, lo:hi], starting_head[:, lo:hi].astype(f32), recharge[None, lo:hi]], axis=0
        )

    top_rows = jnp.moveaxis(stack_rows(0, width), 1, 0)
    bottom_rows = jnp.moveaxis(stack_rows(row_count - width, row_count), 1, 0)
    from_above = jnp.moveaxis(send(bottom_rows, "row", True), 0, 1)
    from_below = jnp.moveaxis(send(top_rows, "row", False), 0, 1)
    stacked_total = from_above.shape[0]
    halo_rows = jnp.concatenate(
        [from_below, jnp.zeros((stacked_total, 8 - 2 * width, col_count), f32), from_above], axis=1
    )

    def stack_cols(lo, hi):
        interior = jnp.concatenate(
            [logarithmic_conductivity[:, :, lo:hi], starting_head[:, :, lo:hi].astype(f32), recharge[None, :, lo:hi]],
            axis=0,
        )
        return jnp.moveaxis(jnp.concatenate([interior, halo_rows[:, :, lo:hi]], axis=1), 2, 0)

    from_left = jnp.moveaxis(send(stack_cols(col_count - width, col_count), "col", True), 0, 2)
    from_right = jnp.moveaxis(send(stack_cols(0, width), "col", False), 0, 2)
    halo_cols = jnp.concatenate(
        [from_right, jnp.zeros((stacked_total, ext_rows, col_count - 2 * width), f32), from_left], axis=2
    )
    inside = circular_inside("row", row_count, width, ext_rows)[:, None] & circular_inside(
        "col", col_count, width, ext_cols
    )[None, :]
    pressure_low, hydraulic_head = run_stencil(
        inside.astype(f32), recharge, halo_rows, halo_cols, logarithmic_conductivity, starting_head, 8
    )
    flat_press = hydraulic_head.reshape(member_count, row_count * col_count)
    group_total, well_count = well_cells.shape
    local_data = jnp.take(flat_press, well_cells.reshape(-1), axis=1)
    me = lax.axis_index("row") * lax.axis_size("col") + lax.axis_index("col")
    mine = jnp.repeat(well_owner == me, well_count)
    local_data = jnp.where(mine[None, :], local_data, 0.0)
    packed = local_data.reshape(-1, 128)
    predicted = butterfly(butterfly(packed, "col"), "row").reshape(local_data.shape)
    mixing = blending_weights(predicted, observed, obs_var, perturb)
    ensemble_spread = math.sqrt(member_count - 1)
    anomalies = (
        logarithmic_conductivity - jnp.mean(logarithmic_conductivity, axis=0, keepdims=True)
    ) / ensemble_spread
    updated_perm = logarithmic_conductivity + jnp.einsum(
        "mrc,mn->nrc", anomalies, mixing, precision=lax.Precision.HIGHEST
    )
    return (pressure_low, predicted, updated_perm)


def solution(mesh):
    return jax.shard_map(
        per_device,
        mesh=mesh,
        in_specs=(
            P(None, "row", "col"),
            P(None, "row", "col"),
            P("row", "col"),
            P(),
            P(),
            P(),
            P(),
            P(),
        ),
        out_specs=(P(None, "row", "col"), P(), P(None, "row", "col")),
        check_vma=False,
    )
```

```python
import math

import jax
import jax.numpy as jnp
from jax import lax
from jax.sharding import PartitionSpec as P
from jax.experimental import pallas as pl
from jax.experimental.pallas import tpu as pltpu

STEPS = 3


time_step = 0.13


def send(piece, axis, forward):
    count = lax.axis_size(axis)
    pairs = [(i, i + 1) for i in range(count - 1)]
    if not forward:
        pairs = [(target, source) for source, target in pairs]
    return lax.ppermute(piece, axis, pairs)


def circular_inside(axis, local, width, size):
    index = jnp.arange(size)
    gap = (index >= local + width) & (index < size - width)
    local_index = jnp.where(index < local + width, index, index - size)
    global_index = lax.axis_index(axis) * local + local_index
    return (~gap) & (global_index >= 0) & (global_index < local * lax.axis_size(axis))


def stencil_kernel(mask_ref, source_ref, source_rows_ref, source_cols_ref, perm_ref, head_ref,
                   perm_rows_ref, head_rows_ref, perm_cols_ref, head_cols_ref, out16_ref, out32_ref):
    rows, cols = perm_ref.shape[1], perm_ref.shape[2]
    ext_rows, ext_cols = rows + 8, 2 * cols

    def extend(interior, halo_rows, halo_cols):
        return jnp.concatenate([jnp.concatenate([interior, halo_rows], axis=0), halo_cols], axis=1)

    inside = mask_ref[...] > 0.5
    source = extend(source_ref[...], source_rows_ref[0], source_cols_ref[0])

    def member(j, carry):
        perm = extend(perm_ref[j], perm_rows_ref[j], perm_cols_ref[j])
        head = extend(head_ref[j].astype(jnp.float32), head_rows_ref[j], head_cols_ref[j])
        vertical = jnp.exp(0.5 * (perm + pltpu.roll(perm, ext_rows - 1, 0)))
        horizontal = jnp.exp(0.5 * (perm + pltpu.roll(perm, ext_cols - 1, 1)))
        faces = (pltpu.roll(vertical, 1, 0), vertical, pltpu.roll(horizontal, 1, 1), horizontal)
        for _ in range(STEPS):
            near = (pltpu.roll(head, 1, 0), pltpu.roll(head, ext_rows - 1, 0),
                    pltpu.roll(head, 1, 1), pltpu.roll(head, ext_cols - 1, 1))
            flux_total = jnp.zeros_like(head)
            for weight_face, near_press in zip(faces, near):
                flux_total = flux_total + weight_face * (near_press - head)
            head = head + time_step * (flux_total + source)
            head = jnp.where(inside, head, 0.0)
        final = head[:rows, :cols]
        out32_ref[j] = final
        out16_ref[j] = final.astype(jnp.bfloat16)
        return carry

    lax.fori_loop(0, perm_ref.shape[0], member, 0)


def run_stencil(mask, source, halo_rows, halo_cols, perm, head, block):
    members, rows, cols = perm.shape
    blocks = members // block
    full2 = lambda shape: pl.BlockSpec(shape, lambda i: (0, 0))
    member_block = lambda shape, shift: pl.BlockSpec((block,) + shape, lambda i: (i + shift, 0, 0))
    last = lambda shape: pl.BlockSpec((1,) + shape, lambda i: (2 * members, 0, 0))
    ext_rows = rows + 8
    cells = members * ext_rows * 2 * cols
    return pl.pallas_call(
        stencil_kernel,
        grid=(blocks,),
        in_specs=[
            full2(mask.shape),
            full2(source.shape),
            last((8, cols)),
            last((ext_rows, cols)),
            member_block((rows, cols), 0),
            member_block((rows, cols), 0),
            member_block((8, cols), 0),
            member_block((8, cols), blocks),
            member_block((ext_rows, cols), 0),
            member_block((ext_rows, cols), blocks),
        ],
        out_specs=[member_block((rows, cols), 0), member_block((rows, cols), 0)],
        out_shape=[
            jax.ShapeDtypeStruct(perm.shape, jnp.bfloat16),
            jax.ShapeDtypeStruct(perm.shape, jnp.float32),
        ],
        cost_estimate=pl.CostEstimate(
            flops=cells * 80, transcendentals=cells * 2, bytes_accessed=members * rows * cols * 14
        ),
    )(mask, source, halo_rows, halo_cols, perm, head, halo_rows, halo_rows, halo_cols, halo_cols)


def broadcast_from_owners(value, axes):
    count = 1
    for axis in axes:
        count *= lax.axis_size(axis)
    chunks = value.reshape(count, -1)
    own_chunk = lax.all_to_all(chunks, axes, 0, 0, tiled=True).sum(axis=0)
    spread = jnp.broadcast_to(own_chunk[None], chunks.shape)
    return lax.all_to_all(spread, axes, 0, 0, tiled=True).reshape(value.shape)


def neighbours(padded):
    return (padded[:, :-2, 1:-1], padded[:, 2:, 1:-1], padded[:, 1:-1, :-2], padded[:, 1:-1, 2:])


def face_terms(padded_perm):
    centre_perm = padded_perm[:, 1:-1, 1:-1]
    return [jnp.exp(0.5 * (centre_perm + near_perm)) for near_perm in neighbours(padded_perm)]


def advance(coefficients, bordered_head, source):
    centre_press = bordered_head[:, 1:-1, 1:-1]
    flux_total = jnp.zeros_like(centre_press)
    for weight_face, near_press in zip(coefficients, neighbours(bordered_head)):
        flux_total = flux_total + weight_face * (near_press - centre_press)
    return centre_press + time_step * (flux_total + source)


def blending_weights(predicted, observed, obs_var, perturb):
    member_count = predicted.shape[0]
    ensemble_spread = math.sqrt(member_count - 1)
    centred = (predicted - jnp.mean(predicted, axis=0, keepdims=True)) / ensemble_spread
    innovation = observed[None, :] + jnp.sqrt(obs_var)[None, :] * perturb - predicted
    weighted = centred / obs_var[None, :]
    system = jnp.eye(member_count, dtype=centred.dtype) + jnp.dot(
        weighted, centred.T, precision=lax.Precision.HIGHEST
    )
    right_side = jnp.dot(weighted, innovation.T, precision=lax.Precision.HIGHEST)
    factor = jnp.linalg.cholesky(system)
    half_solved = lax.linalg.triangular_solve(factor, right_side, left_side=True, lower=True)
    return lax.linalg.triangular_solve(
        factor, half_solved, left_side=True, lower=True, transpose_a=True
    )


def per_device(
    logarithmic_conductivity,
    starting_head,
    recharge,
    well_cells,
    well_owner,
    observed,
    obs_var,
    perturb,
):
    member_count, row_count, col_count = logarithmic_conductivity.shape
    width = STEPS
    ext_rows, ext_cols = row_count + 8, 2 * col_count
    f32 = jnp.float32

    def stack_rows(lo, hi):
        return jnp.concatenate(
            [logarithmic_conductivity[:, lo:hi], starting_head[:, lo:hi].astype(f32), recharge[None, lo:hi]], axis=0
        )

    top_rows = jnp.moveaxis(stack_rows(0, width), 1, 0)
    bottom_rows = jnp.moveaxis(stack_rows(row_count - width, row_count), 1, 0)
    from_above = jnp.moveaxis(send(bottom_rows, "row", True), 0, 1)
    from_below = jnp.moveaxis(send(top_rows, "row", False), 0, 1)
    stacked_total = from_above.shape[0]
    halo_rows = jnp.concatenate(
        [from_below, jnp.zeros((stacked_total, 8 - 2 * width, col_count), f32), from_above], axis=1
    )

    def stack_cols(lo, hi):
        interior = jnp.concatenate(
            [logarithmic_conductivity[:, :, lo:hi], starting_head[:, :, lo:hi].astype(f32), recharge[None, :, lo:hi]],
            axis=0,
        )
        return jnp.moveaxis(jnp.concatenate([interior, halo_rows[:, :, lo:hi]], axis=1), 2, 0)

    from_left = jnp.moveaxis(send(stack_cols(col_count - width, col_count), "col", True), 0, 2)
    from_right = jnp.moveaxis(send(stack_cols(0, width), "col", False), 0, 2)
    halo_cols = jnp.concatenate(
        [from_right, jnp.zeros((stacked_total, ext_rows, col_count - 2 * width), f32), from_left], axis=2
    )
    inside = circular_inside("row", row_count, width, ext_rows)[:, None] & circular_inside(
        "col", col_count, width, ext_cols
    )[None, :]
    pressure_low, hydraulic_head = run_stencil(
        inside.astype(f32), recharge, halo_rows, halo_cols, logarithmic_conductivity, starting_head, 8
    )
    group_total, well_count = well_cells.shape
    wells = well_cells.reshape(-1)
    local_data = hydraulic_head[:, wells // col_count, wells % col_count]
    me = lax.axis_index("row") * lax.axis_size("col") + lax.axis_index("col")
    mine = jnp.repeat(well_owner == me, well_count)
    local_data = jnp.where(mine[None, :], local_data, 0.0)
    predicted = broadcast_from_owners(local_data, ("row", "col"))
    mixing = blending_weights(predicted, observed, obs_var, perturb)
    ensemble_spread = math.sqrt(member_count - 1)
    anomalies = (
        logarithmic_conductivity - jnp.mean(logarithmic_conductivity, axis=0, keepdims=True)
    ) / ensemble_spread
    updated_perm = logarithmic_conductivity + jnp.einsum(
        "mrc,mn->nrc", anomalies, mixing, precision=lax.Precision.HIGHEST
    )
    return (pressure_low, predicted, updated_perm)


def solution(mesh):
    return jax.shard_map(
        per_device,
        mesh=mesh,
        in_specs=(
            P(None, "row", "col"),
            P(None, "row", "col"),
            P("row", "col"),
            P(),
            P(),
            P(),
            P(),
            P(),
        ),
        out_specs=(P(None, "row", "col"), P(), P(None, "row", "col")),
        check_vma=False,
    )
```

```python
import math

import jax
import jax.numpy as jnp
from jax import lax
from jax.sharding import PartitionSpec as P
from jax.experimental import pallas as pl
from jax.experimental.pallas import tpu as pltpu

STEPS = 3


time_step = 0.13


def send(piece, rows_by, cols_by, carried):
    row_count, col_count = lax.axis_size("row"), lax.axis_size("col")
    pairs = []
    for r in range(row_count):
        for c in range(col_count):
            if 0 <= r + rows_by < row_count and 0 <= c + cols_by < col_count:
                pairs.append((r * col_count + c, (r + rows_by) * col_count + c + cols_by))
    if carried:
        moved = jnp.moveaxis(piece, carried, 0)
        return jnp.moveaxis(lax.ppermute(moved, ("row", "col"), pairs), 0, carried)
    moved = jnp.moveaxis(piece, 0, -1)
    return jnp.moveaxis(lax.ppermute(moved, ("row", "col"), pairs), -1, 0)


def circular_inside(axis, local, width, size):
    index = jnp.arange(size)
    gap = (index >= local + width) & (index < size - width)
    local_index = jnp.where(index < local + width, index, index - size)
    global_index = lax.axis_index(axis) * local + local_index
    return (~gap) & (global_index >= 0) & (global_index < local * lax.axis_size(axis))


def stencil_kernel(mask_ref, source_ref, source_rows_ref, source_cols_ref, perm_ref, head_ref,
                   perm_rows_ref, head_rows_ref, perm_cols_ref, head_cols_ref, out16_ref, out32_ref):
    rows, cols = perm_ref.shape[1], perm_ref.shape[2]
    ext_rows, ext_cols = rows + 8, 2 * cols

    def extend(interior, halo_rows, halo_cols):
        return jnp.concatenate([jnp.concatenate([interior, halo_rows], axis=0), halo_cols], axis=1)

    inside = mask_ref[...] > 0.5
    source = extend(source_ref[...], source_rows_ref[0], source_cols_ref[0])

    def member(j, carry):
        perm = extend(perm_ref[j], perm_rows_ref[j], perm_cols_ref[j])
        head = extend(head_ref[j].astype(jnp.float32), head_rows_ref[j], head_cols_ref[j])
        vertical = jnp.exp(0.5 * (perm + pltpu.roll(perm, ext_rows - 1, 0)))
        horizontal = jnp.exp(0.5 * (perm + pltpu.roll(perm, ext_cols - 1, 1)))
        faces = (pltpu.roll(vertical, 1, 0), vertical, pltpu.roll(horizontal, 1, 1), horizontal)
        for _ in range(STEPS):
            near = (pltpu.roll(head, 1, 0), pltpu.roll(head, ext_rows - 1, 0),
                    pltpu.roll(head, 1, 1), pltpu.roll(head, ext_cols - 1, 1))
            flux_total = jnp.zeros_like(head)
            for weight_face, near_press in zip(faces, near):
                flux_total = flux_total + weight_face * (near_press - head)
            head = head + time_step * (flux_total + source)
            head = jnp.where(inside, head, 0.0)
        final = head[:rows, :cols]
        out32_ref[j] = final
        out16_ref[j] = final.astype(jnp.bfloat16)
        return carry

    lax.fori_loop(0, perm_ref.shape[0], member, 0)


def run_stencil(mask, source, halo_rows, halo_cols, perm, head, block):
    members, rows, cols = perm.shape
    blocks = members // block
    full2 = lambda shape: pl.BlockSpec(shape, lambda i: (0, 0))
    member_block = lambda shape, shift: pl.BlockSpec((block,) + shape, lambda i: (i + shift, 0, 0))
    last = lambda shape: pl.BlockSpec((1,) + shape, lambda i: (2 * members, 0, 0))
    ext_rows = rows + 8
    cells = members * ext_rows * 2 * cols
    return pl.pallas_call(
        stencil_kernel,
        grid=(blocks,),
        in_specs=[
            full2(mask.shape),
            full2(source.shape),
            last((8, cols)),
            last((ext_rows, cols)),
            member_block((rows, cols), 0),
            member_block((rows, cols), 0),
            member_block((8, cols), 0),
            member_block((8, cols), blocks),
            member_block((ext_rows, cols), 0),
            member_block((ext_rows, cols), blocks),
        ],
        out_specs=[member_block((rows, cols), 0), member_block((rows, cols), 0)],
        out_shape=[
            jax.ShapeDtypeStruct(perm.shape, jnp.bfloat16),
            jax.ShapeDtypeStruct(perm.shape, jnp.float32),
        ],
        cost_estimate=pl.CostEstimate(
            flops=cells * 80, transcendentals=cells * 2, bytes_accessed=members * rows * cols * 14
        ),
    )(mask, source, halo_rows, halo_cols, perm, head, halo_rows, halo_rows, halo_cols, halo_cols)


def broadcast_from_owners(value, axes):
    count = 1
    for axis in axes:
        count *= lax.axis_size(axis)
    chunks = value.reshape(count, -1)
    own_chunk = lax.all_to_all(chunks, axes, 0, 0, tiled=True).sum(axis=0)
    spread = jnp.broadcast_to(own_chunk[None], chunks.shape)
    return lax.all_to_all(spread, axes, 0, 0, tiled=True).reshape(value.shape)


def neighbours(padded):
    return (padded[:, :-2, 1:-1], padded[:, 2:, 1:-1], padded[:, 1:-1, :-2], padded[:, 1:-1, 2:])


def face_terms(padded_perm):
    centre_perm = padded_perm[:, 1:-1, 1:-1]
    return [jnp.exp(0.5 * (centre_perm + near_perm)) for near_perm in neighbours(padded_perm)]


def advance(coefficients, bordered_head, source):
    centre_press = bordered_head[:, 1:-1, 1:-1]
    flux_total = jnp.zeros_like(centre_press)
    for weight_face, near_press in zip(coefficients, neighbours(bordered_head)):
        flux_total = flux_total + weight_face * (near_press - centre_press)
    return centre_press + time_step * (flux_total + source)


def blending_weights(predicted, observed, obs_var, perturb):
    member_count = predicted.shape[0]
    ensemble_spread = math.sqrt(member_count - 1)
    centred = (predicted - jnp.mean(predicted, axis=0, keepdims=True)) / ensemble_spread
    innovation = observed[None, :] + jnp.sqrt(obs_var)[None, :] * perturb - predicted
    weighted = centred / obs_var[None, :]
    system = jnp.eye(member_count, dtype=centred.dtype) + jnp.dot(
        weighted, centred.T, precision=lax.Precision.HIGHEST
    )
    right_side = jnp.dot(weighted, innovation.T, precision=lax.Precision.HIGHEST)
    factor = jnp.linalg.cholesky(system)
    half_solved = lax.linalg.triangular_solve(factor, right_side, left_side=True, lower=True)
    return lax.linalg.triangular_solve(
        factor, half_solved, left_side=True, lower=True, transpose_a=True
    )


def per_device(
    logarithmic_conductivity,
    starting_head,
    recharge,
    well_cells,
    well_owner,
    observed,
    obs_var,
    perturb,
):
    member_count, row_count, col_count = logarithmic_conductivity.shape
    width = STEPS
    ext_rows, ext_cols = row_count + 8, 2 * col_count
    f32 = jnp.float32

    def piece(rows, cols):
        return jnp.concatenate(
            [
                logarithmic_conductivity[:, rows, cols],
                starting_head[:, rows, cols].astype(f32),
                recharge[None, rows, cols],
            ],
            axis=0,
        )

    first, last, every = slice(0, width), slice(-width, None), slice(None)
    from_above = send(piece(last, every), 1, 0, 1)
    from_below = send(piece(first, every), -1, 0, 1)
    from_left = send(piece(every, last), 0, 1, 2)
    from_right = send(piece(every, first), 0, -1, 2)
    above_left = send(piece(last, last), 1, 1, 0)
    above_right = send(piece(last, first), 1, -1, 0)
    below_left = send(piece(first, last), -1, 1, 0)
    below_right = send(piece(first, first), -1, -1, 0)
    stacked_total = from_above.shape[0]
    gap_rows = 8 - 2 * width
    halo_rows = jnp.concatenate(
        [from_below, jnp.zeros((stacked_total, gap_rows, col_count), f32), from_above], axis=1
    )
    gap_block = jnp.zeros((stacked_total, gap_rows, width), f32)
    right_cols = jnp.concatenate([from_right, below_right, gap_block, above_right], axis=1)
    left_cols = jnp.concatenate([from_left, below_left, gap_block, above_left], axis=1)
    halo_cols = jnp.concatenate(
        [right_cols, jnp.zeros((stacked_total, ext_rows, col_count - 2 * width), f32), left_cols], axis=2
    )
    inside = circular_inside("row", row_count, width, ext_rows)[:, None] & circular_inside(
        "col", col_count, width, ext_cols
    )[None, :]
    pressure_low, hydraulic_head = run_stencil(
        inside.astype(f32), recharge, halo_rows, halo_cols, logarithmic_conductivity, starting_head, 8
    )
    group_total, well_count = well_cells.shape
    local_data = jnp.take(hydraulic_head.reshape(member_count, row_count * col_count), well_cells.reshape(-1), axis=1)
    me = lax.axis_index("row") * lax.axis_size("col") + lax.axis_index("col")
    mine = jnp.repeat(well_owner == me, well_count)
    local_data = jnp.where(mine[None, :], local_data, 0.0)
    predicted = broadcast_from_owners(local_data, ("row", "col"))
    mixing = blending_weights(predicted, observed, obs_var, perturb)
    ensemble_spread = math.sqrt(member_count - 1)
    anomalies = (
        logarithmic_conductivity - jnp.mean(logarithmic_conductivity, axis=0, keepdims=True)
    ) / ensemble_spread
    updated_perm = logarithmic_conductivity + jnp.einsum(
        "mrc,mn->nrc", anomalies, mixing, precision=lax.Precision.HIGHEST
    )
    return (pressure_low, predicted, updated_perm)


def solution(mesh):
    return jax.shard_map(
        per_device,
        mesh=mesh,
        in_specs=(
            P(None, "row", "col"),
            P(None, "row", "col"),
            P("row", "col"),
            P(),
            P(),
            P(),
            P(),
            P(),
        ),
        out_specs=(P(None, "row", "col"), P(), P(None, "row", "col")),
        check_vma=False,
    )
```

```python
import math

import jax
import jax.numpy as jnp
from jax import lax
from jax.sharding import PartitionSpec as P
from jax.experimental import pallas as pl
from jax.experimental.pallas import tpu as pltpu

STEPS = 3


time_step = 0.13


def send(piece, axis, forward):
    count = lax.axis_size(axis)
    pairs = [(i, i + 1) for i in range(count - 1)]
    if not forward:
        pairs = [(target, source) for source, target in pairs]
    return lax.ppermute(piece, axis, pairs)


def circular_inside(axis, local, width, size):
    index = jnp.arange(size)
    gap = (index >= local + width) & (index < size - width)
    local_index = jnp.where(index < local + width, index, index - size)
    global_index = lax.axis_index(axis) * local + local_index
    return (~gap) & (global_index >= 0) & (global_index < local * lax.axis_size(axis))


def stencil_kernel(mask_ref, source_ref, source_rows_ref, source_cols_ref, perm_ref, head_ref,
                   perm_rows_ref, head_rows_ref, perm_cols_ref, head_cols_ref, out16_ref, out32_ref):
    rows, cols = perm_ref.shape[1], perm_ref.shape[2]
    ext_rows, ext_cols = rows + 8, 2 * cols

    def extend(interior, halo_rows, halo_cols):
        return jnp.concatenate([jnp.concatenate([interior, halo_rows], axis=0), halo_cols], axis=1)

    inside = mask_ref[...] > 0.5
    source = extend(source_ref[...], source_rows_ref[0], source_cols_ref[0])

    def member(j, carry):
        perm = extend(perm_ref[j], perm_rows_ref[j], perm_cols_ref[j])
        head = extend(head_ref[j].astype(jnp.float32), head_rows_ref[j], head_cols_ref[j])
        vertical = jnp.exp(0.5 * (perm + pltpu.roll(perm, ext_rows - 1, 0)))
        horizontal = jnp.exp(0.5 * (perm + pltpu.roll(perm, ext_cols - 1, 1)))
        faces = (pltpu.roll(vertical, 1, 0), vertical, pltpu.roll(horizontal, 1, 1), horizontal)
        for _ in range(STEPS):
            near = (pltpu.roll(head, 1, 0), pltpu.roll(head, ext_rows - 1, 0),
                    pltpu.roll(head, 1, 1), pltpu.roll(head, ext_cols - 1, 1))
            flux_total = jnp.zeros_like(head)
            for weight_face, near_press in zip(faces, near):
                flux_total = flux_total + weight_face * (near_press - head)
            head = head + time_step * (flux_total + source)
            head = jnp.where(inside, head, 0.0)
        final = head[:rows, :cols]
        out32_ref[j] = final
        out16_ref[j] = final.astype(jnp.bfloat16)
        return carry

    lax.fori_loop(0, perm_ref.shape[0], member, 0)


def run_stencil(mask, source, halo_rows, halo_cols, perm, head, block):
    members, rows, cols = perm.shape
    blocks = members // block
    full2 = lambda shape: pl.BlockSpec(shape, lambda i: (0, 0))
    member_block = lambda shape, shift: pl.BlockSpec((block,) + shape, lambda i: (i + shift, 0, 0))
    last = lambda shape: pl.BlockSpec((1,) + shape, lambda i: (2 * members, 0, 0))
    ext_rows = rows + 8
    cells = members * ext_rows * 2 * cols
    return pl.pallas_call(
        stencil_kernel,
        grid=(blocks,),
        in_specs=[
            full2(mask.shape),
            full2(source.shape),
            last((8, cols)),
            last((ext_rows, cols)),
            member_block((rows, cols), 0),
            member_block((rows, cols), 0),
            member_block((8, cols), 0),
            member_block((8, cols), blocks),
            member_block((ext_rows, cols), 0),
            member_block((ext_rows, cols), blocks),
        ],
        out_specs=[member_block((rows, cols), 0), member_block((rows, cols), 0)],
        out_shape=[
            jax.ShapeDtypeStruct(perm.shape, jnp.bfloat16),
            jax.ShapeDtypeStruct(perm.shape, jnp.float32),
        ],
        cost_estimate=pl.CostEstimate(
            flops=cells * 80, transcendentals=cells * 2, bytes_accessed=members * rows * cols * 14
        ),
    )(mask, source, halo_rows, halo_cols, perm, head, halo_rows, halo_rows, halo_cols, halo_cols)


def broadcast_from_owners(value, axes):
    count = 1
    for axis in axes:
        count *= lax.axis_size(axis)
    chunks = value.reshape(count, -1)
    own_chunk = lax.all_to_all(chunks, axes, 0, 0, tiled=True).sum(axis=0)
    spread = jnp.broadcast_to(own_chunk[None], chunks.shape)
    return lax.all_to_all(spread, axes, 0, 0, tiled=True).reshape(value.shape)


def neighbours(padded):
    return (padded[:, :-2, 1:-1], padded[:, 2:, 1:-1], padded[:, 1:-1, :-2], padded[:, 1:-1, 2:])


def face_terms(padded_perm):
    centre_perm = padded_perm[:, 1:-1, 1:-1]
    return [jnp.exp(0.5 * (centre_perm + near_perm)) for near_perm in neighbours(padded_perm)]


def advance(coefficients, bordered_head, source):
    centre_press = bordered_head[:, 1:-1, 1:-1]
    flux_total = jnp.zeros_like(centre_press)
    for weight_face, near_press in zip(coefficients, neighbours(bordered_head)):
        flux_total = flux_total + weight_face * (near_press - centre_press)
    return centre_press + time_step * (flux_total + source)


def blending_weights(predicted, observed, obs_var, perturb):
    member_count = predicted.shape[0]
    ensemble_spread = math.sqrt(member_count - 1)
    centred = (predicted - jnp.mean(predicted, axis=0, keepdims=True)) / ensemble_spread
    innovation = observed[None, :] + jnp.sqrt(obs_var)[None, :] * perturb - predicted
    weighted = centred / obs_var[None, :]
    system = jnp.eye(member_count, dtype=centred.dtype) + jnp.dot(
        weighted, centred.T, precision=lax.Precision.HIGHEST
    )
    right_side = jnp.dot(weighted, innovation.T, precision=lax.Precision.HIGHEST)
    factor = jnp.linalg.cholesky(system)
    half_solved = lax.linalg.triangular_solve(factor, right_side, left_side=True, lower=True)
    return lax.linalg.triangular_solve(
        factor, half_solved, left_side=True, lower=True, transpose_a=True
    )


def per_device(
    logarithmic_conductivity,
    starting_head,
    recharge,
    well_cells,
    well_owner,
    observed,
    obs_var,
    perturb,
):
    member_count, row_count, col_count = logarithmic_conductivity.shape
    width = STEPS
    ext_rows, ext_cols = row_count + 8, 2 * col_count
    f32 = jnp.float32

    def stack_rows(lo, hi):
        return jnp.concatenate(
            [logarithmic_conductivity[:, lo:hi], starting_head[:, lo:hi].astype(f32), recharge[None, lo:hi]], axis=0
        )

    top_rows = jnp.moveaxis(stack_rows(0, width), 1, 0)
    bottom_rows = jnp.moveaxis(stack_rows(row_count - width, row_count), 1, 0)
    from_above = jnp.moveaxis(send(bottom_rows, "row", True), 0, 1)
    from_below = jnp.moveaxis(send(top_rows, "row", False), 0, 1)
    stacked_total = from_above.shape[0]
    halo_rows = jnp.concatenate(
        [from_below, jnp.zeros((stacked_total, 8 - 2 * width, col_count), f32), from_above], axis=1
    )

    def stack_cols(lo, hi):
        interior = jnp.concatenate(
            [logarithmic_conductivity[:, :, lo:hi], starting_head[:, :, lo:hi].astype(f32), recharge[None, :, lo:hi]],
            axis=0,
        )
        return jnp.moveaxis(jnp.concatenate([interior, halo_rows[:, :, lo:hi]], axis=1), 2, 0)

    from_left = jnp.moveaxis(send(stack_cols(col_count - width, col_count), "col", True), 0, 2)
    from_right = jnp.moveaxis(send(stack_cols(0, width), "col", False), 0, 2)
    halo_cols = jnp.concatenate(
        [from_right, jnp.zeros((stacked_total, ext_rows, col_count - 2 * width), f32), from_left], axis=2
    )
    inside = circular_inside("row", row_count, width, ext_rows)[:, None] & circular_inside(
        "col", col_count, width, ext_cols
    )[None, :]
    pressure_low, hydraulic_head = run_stencil(
        inside.astype(f32), recharge, halo_rows, halo_cols, logarithmic_conductivity, starting_head, 8
    )
    group_total, well_count = well_cells.shape
    local_data = jnp.take(hydraulic_head.reshape(member_count, row_count * col_count), well_cells.reshape(-1), axis=1)
    me = lax.axis_index("row") * lax.axis_size("col") + lax.axis_index("col")
    mine = jnp.repeat(well_owner == me, well_count)
    local_data = jnp.where(mine[None, :], local_data, 0.0)
    predicted = broadcast_from_owners(local_data, ("row", "col"))
    mixing = blending_weights(predicted, observed, obs_var, perturb)
    ensemble_spread = math.sqrt(member_count - 1)
    anomalies = (
        logarithmic_conductivity - jnp.mean(logarithmic_conductivity, axis=0, keepdims=True)
    ) / ensemble_spread
    updated_perm = logarithmic_conductivity + jnp.einsum(
        "mrc,mn->nrc", anomalies, mixing, precision=lax.Precision.HIGHEST
    )
    return (pressure_low, predicted, updated_perm)


def solution(mesh):
    return jax.shard_map(
        per_device,
        mesh=mesh,
        in_specs=(
            P(None, "row", "col"),
            P(None, "row", "col"),
            P("row", "col"),
            P(),
            P(),
            P(),
            P(),
            P(),
        ),
        out_specs=(P(None, "row", "col"), P(), P(None, "row", "col")),
        check_vma=False,
    )
```

```python
import math

import jax
import jax.numpy as jnp
from jax import lax
from jax.sharding import PartitionSpec as P
from jax.experimental import pallas as pl
from jax.experimental.pallas import tpu as pltpu

STEPS = 3


time_step = 0.13


def send(piece, axis, forward):
    count = lax.axis_size(axis)
    pairs = [(i, i + 1) for i in range(count - 1)]
    if not forward:
        pairs = [(target, source) for source, target in pairs]
    return lax.ppermute(piece, axis, pairs)


def circular_inside(axis, local, width, size):
    index = jnp.arange(size)
    gap = (index >= local + width) & (index < size - width)
    local_index = jnp.where(index < local + width, index, index - size)
    global_index = lax.axis_index(axis) * local + local_index
    return (~gap) & (global_index >= 0) & (global_index < local * lax.axis_size(axis))


def stencil_kernel(mask_ref, source_ref, source_rows_ref, source_cols_ref, perm_ref, head_ref,
                   perm_rows_ref, head_rows_ref, perm_cols_ref, head_cols_ref, out16_ref, out32_ref):
    rows, cols = perm_ref.shape[1], perm_ref.shape[2]
    ext_rows, ext_cols = rows + 8, 2 * cols

    def extend(interior, halo_rows, halo_cols):
        return jnp.concatenate([jnp.concatenate([interior, halo_rows], axis=0), halo_cols], axis=1)

    inside = mask_ref[...] > 0.5
    source = extend(source_ref[...], source_rows_ref[0], source_cols_ref[0])

    def member(j, carry):
        perm = extend(perm_ref[j], perm_rows_ref[j], perm_cols_ref[j])
        head = extend(head_ref[j].astype(jnp.float32), head_rows_ref[j], head_cols_ref[j])
        vertical = jnp.exp(0.5 * (perm + pltpu.roll(perm, ext_rows - 1, 0)))
        horizontal = jnp.exp(0.5 * (perm + pltpu.roll(perm, ext_cols - 1, 1)))
        faces = (pltpu.roll(vertical, 1, 0), vertical, pltpu.roll(horizontal, 1, 1), horizontal)
        for _ in range(STEPS):
            near = (pltpu.roll(head, 1, 0), pltpu.roll(head, ext_rows - 1, 0),
                    pltpu.roll(head, 1, 1), pltpu.roll(head, ext_cols - 1, 1))
            flux_total = jnp.zeros_like(head)
            for weight_face, near_press in zip(faces, near):
                flux_total = flux_total + weight_face * (near_press - head)
            head = head + time_step * (flux_total + source)
            head = jnp.where(inside, head, 0.0)
        final = head[:rows, :cols]
        out32_ref[j] = final
        out16_ref[j] = final.astype(jnp.bfloat16)
        return carry

    lax.fori_loop(0, perm_ref.shape[0], member, 0)


def run_stencil(mask, source, halo_rows, halo_cols, perm, head, block):
    members, rows, cols = perm.shape
    blocks = members // block
    full2 = lambda shape: pl.BlockSpec(shape, lambda i: (0, 0))
    member_block = lambda shape, shift: pl.BlockSpec((block,) + shape, lambda i: (i + shift, 0, 0))
    last = lambda shape: pl.BlockSpec((1,) + shape, lambda i: (2 * members, 0, 0))
    ext_rows = rows + 8
    cells = members * ext_rows * 2 * cols
    return pl.pallas_call(
        stencil_kernel,
        grid=(blocks,),
        in_specs=[
            full2(mask.shape),
            full2(source.shape),
            last((8, cols)),
            last((ext_rows, cols)),
            member_block((rows, cols), 0),
            member_block((rows, cols), 0),
            member_block((8, cols), 0),
            member_block((8, cols), blocks),
            member_block((ext_rows, cols), 0),
            member_block((ext_rows, cols), blocks),
        ],
        out_specs=[member_block((rows, cols), 0), member_block((rows, cols), 0)],
        out_shape=[
            jax.ShapeDtypeStruct(perm.shape, jnp.bfloat16),
            jax.ShapeDtypeStruct(perm.shape, jnp.float32),
        ],
        cost_estimate=pl.CostEstimate(
            flops=cells * 80, transcendentals=cells * 2, bytes_accessed=members * rows * cols * 14
        ),
    )(mask, source, halo_rows, halo_cols, perm, head, halo_rows, halo_rows, halo_cols, halo_cols)


def broadcast_from_owners(value, axes):
    count = 1
    for axis in axes:
        count *= lax.axis_size(axis)
    chunks = value.reshape(count, -1)
    own_chunk = lax.all_to_all(chunks, axes, 0, 0, tiled=True).sum(axis=0)
    spread = jnp.broadcast_to(own_chunk[None], chunks.shape)
    return lax.all_to_all(spread, axes, 0, 0, tiled=True).reshape(value.shape)


def neighbours(padded):
    return (padded[:, :-2, 1:-1], padded[:, 2:, 1:-1], padded[:, 1:-1, :-2], padded[:, 1:-1, 2:])


def face_terms(padded_perm):
    centre_perm = padded_perm[:, 1:-1, 1:-1]
    return [jnp.exp(0.5 * (centre_perm + near_perm)) for near_perm in neighbours(padded_perm)]


def advance(coefficients, bordered_head, source):
    centre_press = bordered_head[:, 1:-1, 1:-1]
    flux_total = jnp.zeros_like(centre_press)
    for weight_face, near_press in zip(coefficients, neighbours(bordered_head)):
        flux_total = flux_total + weight_face * (near_press - centre_press)
    return centre_press + time_step * (flux_total + source)


def update_kernel(mix_t_ref, perm_ref, out_ref):
    members = mix_t_ref.shape[0]
    rows = perm_ref.shape[0] // members
    mix_t = mix_t_ref[...]
    spread = math.sqrt(members - 1)

    def body(r, carry):
        values = perm_ref[pl.ds(r, members, stride=rows)]
        anomalies = (values - jnp.mean(values, axis=0, keepdims=True)) / spread
        shift = jnp.dot(mix_t, anomalies, precision=lax.Precision.HIGHEST, preferred_element_type=jnp.float32)
        out_ref[pl.ds(r, members, stride=rows)] = values + shift
        return carry

    lax.fori_loop(0, rows, body, 0)


def run_update(perm, mixing):
    members, rows, cols = perm.shape
    flat = perm.reshape(members * rows, cols)
    out = pl.pallas_call(
        update_kernel,
        out_shape=jax.ShapeDtypeStruct(flat.shape, jnp.float32),
        cost_estimate=pl.CostEstimate(
            flops=2 * members * members * rows * cols, transcendentals=0, bytes_accessed=8 * members * rows * cols
        ),
    )(mixing.T, flat)
    return out.reshape(perm.shape)


def blending_weights(predicted, observed, obs_var, perturb):
    member_count = predicted.shape[0]
    ensemble_spread = math.sqrt(member_count - 1)
    centred = (predicted - jnp.mean(predicted, axis=0, keepdims=True)) / ensemble_spread
    innovation = observed[None, :] + jnp.sqrt(obs_var)[None, :] * perturb - predicted
    weighted = centred / obs_var[None, :]
    system = jnp.eye(member_count, dtype=centred.dtype) + jnp.dot(
        weighted, centred.T, precision=lax.Precision.HIGHEST
    )
    right_side = jnp.dot(weighted, innovation.T, precision=lax.Precision.HIGHEST)
    factor = jnp.linalg.cholesky(system)
    half_solved = lax.linalg.triangular_solve(factor, right_side, left_side=True, lower=True)
    return lax.linalg.triangular_solve(
        factor, half_solved, left_side=True, lower=True, transpose_a=True
    )


def per_device(
    logarithmic_conductivity,
    starting_head,
    recharge,
    well_cells,
    well_owner,
    observed,
    obs_var,
    perturb,
):
    member_count, row_count, col_count = logarithmic_conductivity.shape
    width = STEPS
    ext_rows, ext_cols = row_count + 8, 2 * col_count
    f32 = jnp.float32

    def stack_rows(lo, hi):
        return jnp.concatenate(
            [logarithmic_conductivity[:, lo:hi], starting_head[:, lo:hi].astype(f32), recharge[None, lo:hi]], axis=0
        )

    top_rows = jnp.moveaxis(stack_rows(0, width), 1, 0)
    bottom_rows = jnp.moveaxis(stack_rows(row_count - width, row_count), 1, 0)
    from_above = jnp.moveaxis(send(bottom_rows, "row", True), 0, 1)
    from_below = jnp.moveaxis(send(top_rows, "row", False), 0, 1)
    stacked_total = from_above.shape[0]
    halo_rows = jnp.concatenate(
        [from_below, jnp.zeros((stacked_total, 8 - 2 * width, col_count), f32), from_above], axis=1
    )

    def stack_cols(lo, hi):
        interior = jnp.concatenate(
            [logarithmic_conductivity[:, :, lo:hi], starting_head[:, :, lo:hi].astype(f32), recharge[None, :, lo:hi]],
            axis=0,
        )
        return jnp.moveaxis(jnp.concatenate([interior, halo_rows[:, :, lo:hi]], axis=1), 2, 0)

    from_left = jnp.moveaxis(send(stack_cols(col_count - width, col_count), "col", True), 0, 2)
    from_right = jnp.moveaxis(send(stack_cols(0, width), "col", False), 0, 2)
    halo_cols = jnp.concatenate(
        [from_right, jnp.zeros((stacked_total, ext_rows, col_count - 2 * width), f32), from_left], axis=2
    )
    inside = circular_inside("row", row_count, width, ext_rows)[:, None] & circular_inside(
        "col", col_count, width, ext_cols
    )[None, :]
    pressure_low, hydraulic_head = run_stencil(
        inside.astype(f32), recharge, halo_rows, halo_cols, logarithmic_conductivity, starting_head, 8
    )
    group_total, well_count = well_cells.shape
    local_data = jnp.take(hydraulic_head.reshape(member_count, row_count * col_count), well_cells.reshape(-1), axis=1)
    me = lax.axis_index("row") * lax.axis_size("col") + lax.axis_index("col")
    mine = jnp.repeat(well_owner == me, well_count)
    local_data = jnp.where(mine[None, :], local_data, 0.0)
    predicted = broadcast_from_owners(local_data, ("row", "col"))
    mixing = blending_weights(predicted, observed, obs_var, perturb)
    updated_perm = run_update(logarithmic_conductivity, mixing)
    return (pressure_low, predicted, updated_perm)


def solution(mesh):
    return jax.shard_map(
        per_device,
        mesh=mesh,
        in_specs=(
            P(None, "row", "col"),
            P(None, "row", "col"),
            P("row", "col"),
            P(),
            P(),
            P(),
            P(),
            P(),
        ),
        out_specs=(P(None, "row", "col"), P(), P(None, "row", "col")),
        check_vma=False,
    )
```

```python
import math

import jax
import jax.numpy as jnp
from jax import lax
from jax.sharding import PartitionSpec as P
from jax.experimental import pallas as pl
from jax.experimental.pallas import tpu as pltpu

STEPS = 3


time_step = 0.13


def send(piece, axis, forward):
    count = lax.axis_size(axis)
    pairs = [(i, i + 1) for i in range(count - 1)]
    if not forward:
        pairs = [(target, source) for source, target in pairs]
    return lax.ppermute(piece, axis, pairs)


def circular_inside(axis, local, width, size):
    index = jnp.arange(size)
    gap = (index >= local + width) & (index < size - width)
    local_index = jnp.where(index < local + width, index, index - size)
    global_index = lax.axis_index(axis) * local + local_index
    return (~gap) & (global_index >= 0) & (global_index < local * lax.axis_size(axis))


def stencil_kernel(mask_ref, source_ref, source_rows_ref, source_cols_ref, perm_ref, head_ref,
                   perm_rows_ref, head_rows_ref, perm_cols_ref, head_cols_ref, out16_ref, out32_ref):
    rows, cols = perm_ref.shape[1], perm_ref.shape[2]
    ext_rows, ext_cols = rows + 8, 2 * cols

    def extend(interior, halo_rows, halo_cols):
        return jnp.concatenate([jnp.concatenate([interior, halo_rows], axis=0), halo_cols], axis=1)

    inside = mask_ref[...] > 0.5
    source = extend(source_ref[...], source_rows_ref[0], source_cols_ref[0])

    def member(j, carry):
        perm = extend(perm_ref[j], perm_rows_ref[j], perm_cols_ref[j])
        head = extend(head_ref[j].astype(jnp.float32), head_rows_ref[j], head_cols_ref[j])
        vertical = jnp.exp(0.5 * (perm + pltpu.roll(perm, ext_rows - 1, 0)))
        horizontal = jnp.exp(0.5 * (perm + pltpu.roll(perm, ext_cols - 1, 1)))
        faces = (pltpu.roll(vertical, 1, 0), vertical, pltpu.roll(horizontal, 1, 1), horizontal)
        for _ in range(STEPS):
            near = (pltpu.roll(head, 1, 0), pltpu.roll(head, ext_rows - 1, 0),
                    pltpu.roll(head, 1, 1), pltpu.roll(head, ext_cols - 1, 1))
            flux_total = jnp.zeros_like(head)
            for weight_face, near_press in zip(faces, near):
                flux_total = flux_total + weight_face * (near_press - head)
            head = head + time_step * (flux_total + source)
            head = jnp.where(inside, head, 0.0)
        final = head[:rows, :cols]
        out32_ref[j] = final
        out16_ref[j] = final.astype(jnp.bfloat16)
        return carry

    lax.fori_loop(0, perm_ref.shape[0], member, 0)


def run_stencil(mask, source, halo_rows, halo_cols, perm, head, block):
    members, rows, cols = perm.shape
    blocks = members // block
    full2 = lambda shape: pl.BlockSpec(shape, lambda i: (0, 0))
    member_block = lambda shape, shift: pl.BlockSpec((block,) + shape, lambda i: (i + shift, 0, 0))
    last = lambda shape: pl.BlockSpec((1,) + shape, lambda i: (2 * members, 0, 0))
    ext_rows = rows + 8
    cells = members * ext_rows * 2 * cols
    return pl.pallas_call(
        stencil_kernel,
        grid=(blocks,),
        in_specs=[
            full2(mask.shape),
            full2(source.shape),
            last((8, cols)),
            last((ext_rows, cols)),
            member_block((rows, cols), 0),
            member_block((rows, cols), 0),
            member_block((8, cols), 0),
            member_block((8, cols), blocks),
            member_block((ext_rows, cols), 0),
            member_block((ext_rows, cols), blocks),
        ],
        out_specs=[member_block((rows, cols), 0), member_block((rows, cols), 0)],
        out_shape=[
            jax.ShapeDtypeStruct(perm.shape, jnp.bfloat16),
            jax.ShapeDtypeStruct(perm.shape, jnp.float32),
        ],
        cost_estimate=pl.CostEstimate(
            flops=cells * 80, transcendentals=cells * 2, bytes_accessed=members * rows * cols * 14
        ),
    )(mask, source, halo_rows, halo_cols, perm, head, halo_rows, halo_rows, halo_cols, halo_cols)


def broadcast_from_owners(value, axes):
    count = 1
    for axis in axes:
        count *= lax.axis_size(axis)
    chunks = value.reshape(count, -1)
    own_chunk = lax.all_to_all(chunks, axes, 0, 0, tiled=True).sum(axis=0)
    spread = jnp.broadcast_to(own_chunk[None], chunks.shape)
    return lax.all_to_all(spread, axes, 0, 0, tiled=True).reshape(value.shape)


def neighbours(padded):
    return (padded[:, :-2, 1:-1], padded[:, 2:, 1:-1], padded[:, 1:-1, :-2], padded[:, 1:-1, 2:])


def face_terms(padded_perm):
    centre_perm = padded_perm[:, 1:-1, 1:-1]
    return [jnp.exp(0.5 * (centre_perm + near_perm)) for near_perm in neighbours(padded_perm)]


def advance(coefficients, bordered_head, source):
    centre_press = bordered_head[:, 1:-1, 1:-1]
    flux_total = jnp.zeros_like(centre_press)
    for weight_face, near_press in zip(coefficients, neighbours(bordered_head)):
        flux_total = flux_total + weight_face * (near_press - centre_press)
    return centre_press + time_step * (flux_total + source)


def blending_weights(predicted, observed, obs_var, perturb):
    member_count = predicted.shape[0]
    ensemble_spread = math.sqrt(member_count - 1)
    centred = (predicted - jnp.mean(predicted, axis=0, keepdims=True)) / ensemble_spread
    innovation = observed[None, :] + jnp.sqrt(obs_var)[None, :] * perturb - predicted
    weighted = centred / obs_var[None, :]
    system = jnp.eye(member_count, dtype=centred.dtype) + jnp.dot(
        weighted, centred.T, precision=lax.Precision.HIGHEST
    )
    right_side = jnp.dot(weighted, innovation.T, precision=lax.Precision.HIGHEST)
    factor = jnp.linalg.cholesky(system)
    half_solved = lax.linalg.triangular_solve(factor, right_side, left_side=True, lower=True)
    return lax.linalg.triangular_solve(
        factor, half_solved, left_side=True, lower=True, transpose_a=True
    )


def per_device(
    logarithmic_conductivity,
    starting_head,
    recharge,
    well_cells,
    well_owner,
    observed,
    obs_var,
    perturb,
):
    member_count, row_count, col_count = logarithmic_conductivity.shape
    width = STEPS
    ext_rows, ext_cols = row_count + 8, 2 * col_count
    f32 = jnp.float32

    def stack_rows(lo, hi):
        return jnp.concatenate(
            [logarithmic_conductivity[:, lo:hi], starting_head[:, lo:hi].astype(f32), recharge[None, lo:hi]], axis=0
        )

    top_rows = jnp.moveaxis(stack_rows(0, width), 1, 0)
    bottom_rows = jnp.moveaxis(stack_rows(row_count - width, row_count), 1, 0)
    from_above = jnp.moveaxis(send(bottom_rows, "row", True), 0, 1)
    from_below = jnp.moveaxis(send(top_rows, "row", False), 0, 1)
    stacked_total = from_above.shape[0]
    halo_rows = jnp.concatenate(
        [from_below, jnp.zeros((stacked_total, 8 - 2 * width, col_count), f32), from_above], axis=1
    )

    highest = lax.Precision.HIGHEST
    lane = jnp.arange(col_count)
    pick = jnp.arange(8)
    wanted = jnp.where(pick < width, pick, col_count - 8 + pick)
    selector = ((pick[:, None] < width) | (pick[:, None] >= 8 - width)) & (lane[None, :] == wanted[:, None])
    selector = selector.astype(f32)

    def columns(block):
        flat = block.reshape(-1, col_count)
        if block.dtype == jnp.bfloat16:
            return jnp.dot(selector.astype(jnp.bfloat16), flat.T, preferred_element_type=f32)
        return jnp.dot(selector, flat.T, precision=highest)

    interior_cols = jnp.concatenate(
        [
            columns(logarithmic_conductivity).reshape(8, member_count, row_count),
            columns(starting_head).reshape(8, member_count, row_count),
            columns(recharge).reshape(8, 1, row_count),
        ],
        axis=1,
    )
    border_cols = jnp.concatenate([interior_cols, columns(halo_rows).reshape(8, stacked_total, 8)], axis=2)
    from_left = send(border_cols[8 - width :], "col", True)
    from_right = send(border_cols[:width], "col", False)
    received = jnp.concatenate([from_right, jnp.zeros((8 - 2 * width,) + from_right.shape[1:], f32), from_left], axis=0)
    halo_cols = jnp.einsum("kmr,kl->mrl", received, selector, precision=highest)
    inside = circular_inside("row", row_count, width, ext_rows)[:, None] & circular_inside(
        "col", col_count, width, ext_cols
    )[None, :]
    pressure_low, hydraulic_head = run_stencil(
        inside.astype(f32), recharge, halo_rows, halo_cols, logarithmic_conductivity, starting_head, 8
    )
    group_total, well_count = well_cells.shape
    local_data = jnp.take(hydraulic_head.reshape(member_count, row_count * col_count), well_cells.reshape(-1), axis=1)
    me = lax.axis_index("row") * lax.axis_size("col") + lax.axis_index("col")
    mine = jnp.repeat(well_owner == me, well_count)
    local_data = jnp.where(mine[None, :], local_data, 0.0)
    predicted = broadcast_from_owners(local_data, ("row", "col"))
    mixing = blending_weights(predicted, observed, obs_var, perturb)
    ensemble_spread = math.sqrt(member_count - 1)
    anomalies = (
        logarithmic_conductivity - jnp.mean(logarithmic_conductivity, axis=0, keepdims=True)
    ) / ensemble_spread
    updated_perm = logarithmic_conductivity + jnp.einsum(
        "mrc,mn->nrc", anomalies, mixing, precision=lax.Precision.HIGHEST
    )
    return (pressure_low, predicted, updated_perm)


def solution(mesh):
    return jax.shard_map(
        per_device,
        mesh=mesh,
        in_specs=(
            P(None, "row", "col"),
            P(None, "row", "col"),
            P("row", "col"),
            P(),
            P(),
            P(),
            P(),
            P(),
        ),
        out_specs=(P(None, "row", "col"), P(), P(None, "row", "col")),
        check_vma=False,
    )
```

```python
import math

import jax
import jax.numpy as jnp
from jax import lax
from jax.sharding import PartitionSpec as P
from jax.experimental import pallas as pl
from jax.experimental.pallas import tpu as pltpu

STEPS = 3


time_step = 0.13


def send(piece, axis, forward):
    count = lax.axis_size(axis)
    pairs = [(i, i + 1) for i in range(count - 1)]
    if not forward:
        pairs = [(target, source) for source, target in pairs]
    return lax.ppermute(piece, axis, pairs)


def circular_inside(axis, local, width, size):
    index = jnp.arange(size)
    gap = (index >= local + width) & (index < size - width)
    local_index = jnp.where(index < local + width, index, index - size)
    global_index = lax.axis_index(axis) * local + local_index
    return (~gap) & (global_index >= 0) & (global_index < local * lax.axis_size(axis))


def stencil_kernel(mask_ref, source_ref, source_rows_ref, source_cols_ref, perm_ref, head_ref,
                   perm_rows_ref, head_rows_ref, perm_cols_ref, head_cols_ref, out16_ref, out32_ref):
    rows, cols = perm_ref.shape[1], perm_ref.shape[2]
    ext_rows, ext_cols = rows + 8, 2 * cols

    def extend(interior, halo_rows, halo_cols):
        return jnp.concatenate([jnp.concatenate([interior, halo_rows], axis=0), halo_cols], axis=1)

    inside = mask_ref[...] > 0.5
    source = extend(source_ref[...], source_rows_ref[0], source_cols_ref[0])

    def member(j, carry):
        perm = extend(perm_ref[j], perm_rows_ref[j], perm_cols_ref[j])
        head = extend(head_ref[j].astype(jnp.float32), head_rows_ref[j], head_cols_ref[j])
        vertical = jnp.exp(0.5 * (perm + pltpu.roll(perm, ext_rows - 1, 0)))
        horizontal = jnp.exp(0.5 * (perm + pltpu.roll(perm, ext_cols - 1, 1)))
        faces = (pltpu.roll(vertical, 1, 0), vertical, pltpu.roll(horizontal, 1, 1), horizontal)
        for step_index in range(STEPS):
            near = (pltpu.roll(head, 1, 0), pltpu.roll(head, ext_rows - 1, 0),
                    pltpu.roll(head, 1, 1), pltpu.roll(head, ext_cols - 1, 1))
            if step_index == STEPS - 1:
                crop = lambda x: x[:rows, :cols]
                near, weights, centre, src = [crop(x) for x in near], [crop(x) for x in faces], crop(head), crop(source)
            else:
                weights, centre, src = faces, head, source
            flux_total = jnp.zeros_like(centre)
            for weight_face, near_press in zip(weights, near):
                flux_total = flux_total + weight_face * (near_press - centre)
            head = centre + time_step * (flux_total + src)
            if step_index < STEPS - 1:
                head = jnp.where(inside, head, 0.0)
        final = head
        out32_ref[j] = final
        out16_ref[j] = final.astype(jnp.bfloat16)
        return carry

    lax.fori_loop(0, perm_ref.shape[0], member, 0)


def run_stencil(mask, source, halo_rows, halo_cols, perm, head, block):
    members, rows, cols = perm.shape
    blocks = members // block
    full2 = lambda shape: pl.BlockSpec(shape, lambda i: (0, 0))
    member_block = lambda shape, shift: pl.BlockSpec((block,) + shape, lambda i: (i + shift, 0, 0))
    last = lambda shape: pl.BlockSpec((1,) + shape, lambda i: (2 * members, 0, 0))
    ext_rows = rows + 8
    cells = members * ext_rows * 2 * cols
    return pl.pallas_call(
        stencil_kernel,
        grid=(blocks,),
        in_specs=[
            full2(mask.shape),
            full2(source.shape),
            last((8, cols)),
            last((ext_rows, cols)),
            member_block((rows, cols), 0),
            member_block((rows, cols), 0),
            member_block((8, cols), 0),
            member_block((8, cols), blocks),
            member_block((ext_rows, cols), 0),
            member_block((ext_rows, cols), blocks),
        ],
        out_specs=[member_block((rows, cols), 0), member_block((rows, cols), 0)],
        out_shape=[
            jax.ShapeDtypeStruct(perm.shape, jnp.bfloat16),
            jax.ShapeDtypeStruct(perm.shape, jnp.float32),
        ],
        cost_estimate=pl.CostEstimate(
            flops=cells * 80, transcendentals=cells * 2, bytes_accessed=members * rows * cols * 14
        ),
    )(mask, source, halo_rows, halo_cols, perm, head, halo_rows, halo_rows, halo_cols, halo_cols)


def broadcast_from_owners(value, axes):
    count = 1
    for axis in axes:
        count *= lax.axis_size(axis)
    chunks = value.reshape(count, -1)
    own_chunk = lax.all_to_all(chunks, axes, 0, 0, tiled=True).sum(axis=0)
    spread = jnp.broadcast_to(own_chunk[None], chunks.shape)
    return lax.all_to_all(spread, axes, 0, 0, tiled=True).reshape(value.shape)


def neighbours(padded):
    return (padded[:, :-2, 1:-1], padded[:, 2:, 1:-1], padded[:, 1:-1, :-2], padded[:, 1:-1, 2:])


def face_terms(padded_perm):
    centre_perm = padded_perm[:, 1:-1, 1:-1]
    return [jnp.exp(0.5 * (centre_perm + near_perm)) for near_perm in neighbours(padded_perm)]


def advance(coefficients, bordered_head, source):
    centre_press = bordered_head[:, 1:-1, 1:-1]
    flux_total = jnp.zeros_like(centre_press)
    for weight_face, near_press in zip(coefficients, neighbours(bordered_head)):
        flux_total = flux_total + weight_face * (near_press - centre_press)
    return centre_press + time_step * (flux_total + source)


def blending_weights(predicted, observed, obs_var, perturb):
    member_count = predicted.shape[0]
    ensemble_spread = math.sqrt(member_count - 1)
    centred = (predicted - jnp.mean(predicted, axis=0, keepdims=True)) / ensemble_spread
    innovation = observed[None, :] + jnp.sqrt(obs_var)[None, :] * perturb - predicted
    weighted = centred / obs_var[None, :]
    system = jnp.eye(member_count, dtype=centred.dtype) + jnp.dot(
        weighted, centred.T, precision=lax.Precision.HIGHEST
    )
    right_side = jnp.dot(weighted, innovation.T, precision=lax.Precision.HIGHEST)
    factor = jnp.linalg.cholesky(system)
    half_solved = lax.linalg.triangular_solve(factor, right_side, left_side=True, lower=True)
    return lax.linalg.triangular_solve(
        factor, half_solved, left_side=True, lower=True, transpose_a=True
    )


def per_device(
    logarithmic_conductivity,
    starting_head,
    recharge,
    well_cells,
    well_owner,
    observed,
    obs_var,
    perturb,
):
    member_count, row_count, col_count = logarithmic_conductivity.shape
    width = STEPS
    ext_rows, ext_cols = row_count + 8, 2 * col_count
    f32 = jnp.float32

    def stack_rows(lo, hi):
        return jnp.concatenate(
            [logarithmic_conductivity[:, lo:hi], starting_head[:, lo:hi].astype(f32), recharge[None, lo:hi]], axis=0
        )

    top_rows = jnp.moveaxis(stack_rows(0, width), 1, 0)
    bottom_rows = jnp.moveaxis(stack_rows(row_count - width, row_count), 1, 0)
    from_above = jnp.moveaxis(send(bottom_rows, "row", True), 0, 1)
    from_below = jnp.moveaxis(send(top_rows, "row", False), 0, 1)
    stacked_total = from_above.shape[0]
    halo_rows = jnp.concatenate(
        [from_below, jnp.zeros((stacked_total, 8 - 2 * width, col_count), f32), from_above], axis=1
    )

    highest = lax.Precision.HIGHEST
    lane = jnp.arange(col_count)
    pick = jnp.arange(8)
    wanted = jnp.where(pick < width, pick, col_count - 8 + pick)
    selector = ((pick[:, None] < width) | (pick[:, None] >= 8 - width)) & (lane[None, :] == wanted[:, None])
    selector = selector.astype(f32)

    def columns(block):
        flat = block.reshape(-1, col_count)
        if block.dtype == jnp.bfloat16:
            return jnp.dot(selector.astype(jnp.bfloat16), flat.T, preferred_element_type=f32)
        return jnp.dot(selector, flat.T, precision=highest)

    interior_cols = jnp.concatenate(
        [
            columns(logarithmic_conductivity).reshape(8, member_count, row_count),
            columns(starting_head).reshape(8, member_count, row_count),
            columns(recharge).reshape(8, 1, row_count),
        ],
        axis=1,
    )
    border_cols = jnp.concatenate([interior_cols, columns(halo_rows).reshape(8, stacked_total, 8)], axis=2)
    from_left = send(border_cols[8 - width :], "col", True)
    from_right = send(border_cols[:width], "col", False)
    received = jnp.concatenate([from_right, jnp.zeros((8 - 2 * width,) + from_right.shape[1:], f32), from_left], axis=0)
    halo_cols = jnp.einsum("kmr,kl->mrl", received, selector, precision=highest)
    inside = circular_inside("row", row_count, width, ext_rows)[:, None] & circular_inside(
        "col", col_count, width, ext_cols
    )[None, :]
    pressure_low, hydraulic_head = run_stencil(
        inside.astype(f32), recharge, halo_rows, halo_cols, logarithmic_conductivity, starting_head, 8
    )
    group_total, well_count = well_cells.shape
    local_data = jnp.take(hydraulic_head.reshape(member_count, row_count * col_count), well_cells.reshape(-1), axis=1)
    me = lax.axis_index("row") * lax.axis_size("col") + lax.axis_index("col")
    mine = jnp.repeat(well_owner == me, well_count)
    local_data = jnp.where(mine[None, :], local_data, 0.0)
    predicted = broadcast_from_owners(local_data, ("row", "col"))
    mixing = blending_weights(predicted, observed, obs_var, perturb)
    ensemble_spread = math.sqrt(member_count - 1)
    anomalies = (
        logarithmic_conductivity - jnp.mean(logarithmic_conductivity, axis=0, keepdims=True)
    ) / ensemble_spread
    updated_perm = logarithmic_conductivity + jnp.einsum(
        "mrc,mn->nrc", anomalies, mixing, precision=lax.Precision.HIGHEST
    )
    return (pressure_low, predicted, updated_perm)


def solution(mesh):
    return jax.shard_map(
        per_device,
        mesh=mesh,
        in_specs=(
            P(None, "row", "col"),
            P(None, "row", "col"),
            P("row", "col"),
            P(),
            P(),
            P(),
            P(),
            P(),
        ),
        out_specs=(P(None, "row", "col"), P(), P(None, "row", "col")),
        check_vma=False,
    )
```

```python
import math

import jax
import jax.numpy as jnp
from jax import lax
from jax.sharding import PartitionSpec as P
from jax.experimental import pallas as pl
from jax.experimental.pallas import tpu as pltpu

STEPS = 3


time_step = 0.13


def send(piece, axis, forward):
    count = lax.axis_size(axis)
    pairs = [(i, i + 1) for i in range(count - 1)]
    if not forward:
        pairs = [(target, source) for source, target in pairs]
    return lax.ppermute(piece, axis, pairs)


def circular_inside(axis, local, width, size):
    index = jnp.arange(size)
    gap = (index >= local + width) & (index < size - width)
    local_index = jnp.where(index < local + width, index, index - size)
    global_index = lax.axis_index(axis) * local + local_index
    return (~gap) & (global_index >= 0) & (global_index < local * lax.axis_size(axis))


def stencil_kernel(mask_ref, selector_ref, source_ref, source_rows_ref, source_cols_ref, perm_ref, head_ref,
                   perm_rows_ref, head_rows_ref, perm_cols_ref, head_cols_ref, out16_ref, out32_ref):
    rows, cols = perm_ref.shape[1], perm_ref.shape[2]
    ext_rows, ext_cols = rows + 8, 2 * cols

    selector = selector_ref[...]

    def extend(interior, halo_rows, halo_cols):
        placed = lax.dot_general(
            halo_cols, selector, (((0,), (0,)), ((), ())), precision=lax.Precision.HIGHEST,
            preferred_element_type=jnp.float32,
        )
        return jnp.concatenate([jnp.concatenate([interior, halo_rows], axis=0), placed], axis=1)

    inside = mask_ref[...] > 0.5
    source = extend(source_ref[...], source_rows_ref[0], source_cols_ref[0])

    def member(j, carry):
        perm = extend(perm_ref[j], perm_rows_ref[j], perm_cols_ref[j])
        head = extend(head_ref[j].astype(jnp.float32), head_rows_ref[j], head_cols_ref[j])
        vertical = jnp.exp(0.5 * (perm + pltpu.roll(perm, ext_rows - 1, 0)))
        horizontal = jnp.exp(0.5 * (perm + pltpu.roll(perm, ext_cols - 1, 1)))
        faces = (pltpu.roll(vertical, 1, 0), vertical, pltpu.roll(horizontal, 1, 1), horizontal)
        for step_index in range(STEPS):
            near = (pltpu.roll(head, 1, 0), pltpu.roll(head, ext_rows - 1, 0),
                    pltpu.roll(head, 1, 1), pltpu.roll(head, ext_cols - 1, 1))
            if step_index == STEPS - 1:
                crop = lambda x: x[:rows, :cols]
                near, weights, centre, src = [crop(x) for x in near], [crop(x) for x in faces], crop(head), crop(source)
            else:
                weights, centre, src = faces, head, source
            flux_total = jnp.zeros_like(centre)
            for weight_face, near_press in zip(weights, near):
                flux_total = flux_total + weight_face * (near_press - centre)
            head = centre + time_step * (flux_total + src)
            if step_index < STEPS - 1:
                head = jnp.where(inside, head, 0.0)
        final = head
        out32_ref[j] = final
        out16_ref[j] = final.astype(jnp.bfloat16)
        return carry

    lax.fori_loop(0, perm_ref.shape[0], member, 0)


def run_stencil(mask, selector, source, halo_rows, halo_cols, perm, head, block):
    members, rows, cols = perm.shape
    blocks = members // block
    full2 = lambda shape: pl.BlockSpec(shape, lambda i: (0, 0))
    member_block = lambda shape, shift: pl.BlockSpec((block,) + shape, lambda i: (i + shift, 0, 0))
    last = lambda shape: pl.BlockSpec((1,) + shape, lambda i: (2 * members, 0, 0))
    ext_rows = rows + 8
    cells = members * ext_rows * 2 * cols
    return pl.pallas_call(
        stencil_kernel,
        grid=(blocks,),
        in_specs=[
            full2(mask.shape),
            full2(selector.shape),
            full2(source.shape),
            last((8, cols)),
            last((8, ext_rows)),
            member_block((rows, cols), 0),
            member_block((rows, cols), 0),
            member_block((8, cols), 0),
            member_block((8, cols), blocks),
            member_block((8, ext_rows), 0),
            member_block((8, ext_rows), blocks),
        ],
        out_specs=[member_block((rows, cols), 0), member_block((rows, cols), 0)],
        out_shape=[
            jax.ShapeDtypeStruct(perm.shape, jnp.bfloat16),
            jax.ShapeDtypeStruct(perm.shape, jnp.float32),
        ],
        cost_estimate=pl.CostEstimate(
            flops=cells * 80, transcendentals=cells * 2, bytes_accessed=members * rows * cols * 14
        ),
    )(mask, selector, source, halo_rows, halo_cols, perm, head, halo_rows, halo_rows, halo_cols, halo_cols)


def broadcast_from_owners(value, axes):
    count = 1
    for axis in axes:
        count *= lax.axis_size(axis)
    chunks = value.reshape(count, -1)
    own_chunk = lax.all_to_all(chunks, axes, 0, 0, tiled=True).sum(axis=0)
    spread = jnp.broadcast_to(own_chunk[None], chunks.shape)
    return lax.all_to_all(spread, axes, 0, 0, tiled=True).reshape(value.shape)


def neighbours(padded):
    return (padded[:, :-2, 1:-1], padded[:, 2:, 1:-1], padded[:, 1:-1, :-2], padded[:, 1:-1, 2:])


def face_terms(padded_perm):
    centre_perm = padded_perm[:, 1:-1, 1:-1]
    return [jnp.exp(0.5 * (centre_perm + near_perm)) for near_perm in neighbours(padded_perm)]


def advance(coefficients, bordered_head, source):
    centre_press = bordered_head[:, 1:-1, 1:-1]
    flux_total = jnp.zeros_like(centre_press)
    for weight_face, near_press in zip(coefficients, neighbours(bordered_head)):
        flux_total = flux_total + weight_face * (near_press - centre_press)
    return centre_press + time_step * (flux_total + source)


def blending_weights(predicted, observed, obs_var, perturb):
    member_count = predicted.shape[0]
    ensemble_spread = math.sqrt(member_count - 1)
    centred = (predicted - jnp.mean(predicted, axis=0, keepdims=True)) / ensemble_spread
    innovation = observed[None, :] + jnp.sqrt(obs_var)[None, :] * perturb - predicted
    weighted = centred / obs_var[None, :]
    system = jnp.eye(member_count, dtype=centred.dtype) + jnp.dot(
        weighted, centred.T, precision=lax.Precision.HIGHEST
    )
    right_side = jnp.dot(weighted, innovation.T, precision=lax.Precision.HIGHEST)
    factor = jnp.linalg.cholesky(system)
    half_solved = lax.linalg.triangular_solve(factor, right_side, left_side=True, lower=True)
    return lax.linalg.triangular_solve(
        factor, half_solved, left_side=True, lower=True, transpose_a=True
    )


def per_device(
    logarithmic_conductivity,
    starting_head,
    recharge,
    well_cells,
    well_owner,
    observed,
    obs_var,
    perturb,
):
    member_count, row_count, col_count = logarithmic_conductivity.shape
    width = STEPS
    ext_rows, ext_cols = row_count + 8, 2 * col_count
    f32 = jnp.float32

    def stack_rows(lo, hi):
        return jnp.concatenate(
            [logarithmic_conductivity[:, lo:hi], starting_head[:, lo:hi].astype(f32), recharge[None, lo:hi]], axis=0
        )

    top_rows = jnp.moveaxis(stack_rows(0, width), 1, 0)
    bottom_rows = jnp.moveaxis(stack_rows(row_count - width, row_count), 1, 0)
    from_above = jnp.moveaxis(send(bottom_rows, "row", True), 0, 1)
    from_below = jnp.moveaxis(send(top_rows, "row", False), 0, 1)
    stacked_total = from_above.shape[0]
    halo_rows = jnp.concatenate(
        [from_below, jnp.zeros((stacked_total, 8 - 2 * width, col_count), f32), from_above], axis=1
    )

    highest = lax.Precision.HIGHEST
    lane = jnp.arange(col_count)
    pick = jnp.arange(8)
    wanted = jnp.where(pick < width, pick, col_count - 8 + pick)
    selector = ((pick[:, None] < width) | (pick[:, None] >= 8 - width)) & (lane[None, :] == wanted[:, None])
    selector = selector.astype(f32)

    def columns(block):
        flat = block.reshape(-1, col_count)
        if block.dtype == jnp.bfloat16:
            return jnp.dot(selector.astype(jnp.bfloat16), flat.T, preferred_element_type=f32)
        return jnp.dot(selector, flat.T, precision=highest)

    interior_cols = jnp.concatenate(
        [
            columns(logarithmic_conductivity).reshape(8, member_count, row_count),
            columns(starting_head).reshape(8, member_count, row_count),
            columns(recharge).reshape(8, 1, row_count),
        ],
        axis=1,
    )
    border_cols = jnp.concatenate([interior_cols, columns(halo_rows).reshape(8, stacked_total, 8)], axis=2)
    from_left = send(border_cols[8 - width :], "col", True)
    from_right = send(border_cols[:width], "col", False)
    received = jnp.concatenate([from_right, jnp.zeros((8 - 2 * width,) + from_right.shape[1:], f32), from_left], axis=0)
    halo_cols = jnp.moveaxis(received, 0, 1)
    inside = circular_inside("row", row_count, width, ext_rows)[:, None] & circular_inside(
        "col", col_count, width, ext_cols
    )[None, :]
    pressure_low, hydraulic_head = run_stencil(
        inside.astype(f32), selector, recharge, halo_rows, halo_cols, logarithmic_conductivity, starting_head, 8
    )
    group_total, well_count = well_cells.shape
    local_data = jnp.take(hydraulic_head.reshape(member_count, row_count * col_count), well_cells.reshape(-1), axis=1)
    me = lax.axis_index("row") * lax.axis_size("col") + lax.axis_index("col")
    mine = jnp.repeat(well_owner == me, well_count)
    local_data = jnp.where(mine[None, :], local_data, 0.0)
    predicted = broadcast_from_owners(local_data, ("row", "col"))
    mixing = blending_weights(predicted, observed, obs_var, perturb)
    ensemble_spread = math.sqrt(member_count - 1)
    anomalies = (
        logarithmic_conductivity - jnp.mean(logarithmic_conductivity, axis=0, keepdims=True)
    ) / ensemble_spread
    updated_perm = logarithmic_conductivity + jnp.einsum(
        "mrc,mn->nrc", anomalies, mixing, precision=lax.Precision.HIGHEST
    )
    return (pressure_low, predicted, updated_perm)


def solution(mesh):
    return jax.shard_map(
        per_device,
        mesh=mesh,
        in_specs=(
            P(None, "row", "col"),
            P(None, "row", "col"),
            P("row", "col"),
            P(),
            P(),
            P(),
            P(),
            P(),
        ),
        out_specs=(P(None, "row", "col"), P(), P(None, "row", "col")),
        check_vma=False,
    )
```

```python
import math

import jax
import jax.numpy as jnp
from jax import lax
from jax.sharding import PartitionSpec as P
from jax.experimental import pallas as pl
from jax.experimental.pallas import tpu as pltpu

STEPS = 3


time_step = 0.13


def send(piece, axis, forward):
    count = lax.axis_size(axis)
    pairs = [(i, i + 1) for i in range(count - 1)]
    if not forward:
        pairs = [(target, source) for source, target in pairs]
    return lax.ppermute(piece, axis, pairs)


def circular_inside(axis, local, width, size):
    index = jnp.arange(size)
    gap = (index >= local + width) & (index < size - width)
    local_index = jnp.where(index < local + width, index, index - size)
    global_index = lax.axis_index(axis) * local + local_index
    return (~gap) & (global_index >= 0) & (global_index < local * lax.axis_size(axis))


def stencil_kernel(mask_ref, source_ref, source_rows_ref, source_cols_ref, perm_ref, head_ref,
                   perm_rows_ref, head_rows_ref, perm_cols_ref, head_cols_ref, out16_ref, out32_ref):
    rows, cols = perm_ref.shape[1], perm_ref.shape[2]
    ext_rows, ext_cols = rows + 8, 2 * cols

    def extend(interior, halo_rows, halo_cols):
        return jnp.concatenate([jnp.concatenate([interior, halo_rows], axis=0), halo_cols], axis=1)

    inside = mask_ref[...] > 0.5
    source = extend(source_ref[...], source_rows_ref[0], source_cols_ref[0])

    def member(j, carry):
        perm = extend(perm_ref[j], perm_rows_ref[j], perm_cols_ref[j])
        head = extend(head_ref[j].astype(jnp.float32), head_rows_ref[j], head_cols_ref[j])
        vertical = jnp.exp(0.5 * (perm + pltpu.roll(perm, ext_rows - 1, 0)))
        horizontal = jnp.exp(0.5 * (perm + pltpu.roll(perm, ext_cols - 1, 1)))
        faces = (pltpu.roll(vertical, 1, 0), vertical, pltpu.roll(horizontal, 1, 1), horizontal)
        for step_index in range(STEPS):
            near = (pltpu.roll(head, 1, 0), pltpu.roll(head, ext_rows - 1, 0),
                    pltpu.roll(head, 1, 1), pltpu.roll(head, ext_cols - 1, 1))
            if step_index == STEPS - 1:
                crop = lambda x: x[:rows, :cols]
                near, weights, centre, src = [crop(x) for x in near], [crop(x) for x in faces], crop(head), crop(source)
            else:
                weights, centre, src = faces, head, source
            flux_total = jnp.zeros_like(centre)
            for weight_face, near_press in zip(weights, near):
                flux_total = flux_total + weight_face * (near_press - centre)
            head = centre + time_step * (flux_total + src)
            if step_index < STEPS - 1:
                head = jnp.where(inside, head, 0.0)
        final = head
        out32_ref[j] = final
        out16_ref[j] = final.astype(jnp.bfloat16)
        return carry

    lax.fori_loop(0, perm_ref.shape[0], member, 0, unroll=2)


def run_stencil(mask, source, halo_rows, halo_cols, perm, head, block):
    members, rows, cols = perm.shape
    blocks = members // block
    full2 = lambda shape: pl.BlockSpec(shape, lambda i: (0, 0))
    member_block = lambda shape, shift: pl.BlockSpec((block,) + shape, lambda i: (i + shift, 0, 0))
    last = lambda shape: pl.BlockSpec((1,) + shape, lambda i: (2 * members, 0, 0))
    ext_rows = rows + 8
    cells = members * ext_rows * 2 * cols
    return pl.pallas_call(
        stencil_kernel,
        grid=(blocks,),
        in_specs=[
            full2(mask.shape),
            full2(source.shape),
            last((8, cols)),
            last((ext_rows, cols)),
            member_block((rows, cols), 0),
            member_block((rows, cols), 0),
            member_block((8, cols), 0),
            member_block((8, cols), blocks),
            member_block((ext_rows, cols), 0),
            member_block((ext_rows, cols), blocks),
        ],
        out_specs=[member_block((rows, cols), 0), member_block((rows, cols), 0)],
        out_shape=[
            jax.ShapeDtypeStruct(perm.shape, jnp.bfloat16),
            jax.ShapeDtypeStruct(perm.shape, jnp.float32),
        ],
        cost_estimate=pl.CostEstimate(
            flops=cells * 80, transcendentals=cells * 2, bytes_accessed=members * rows * cols * 14
        ),
    )(mask, source, halo_rows, halo_cols, perm, head, halo_rows, halo_rows, halo_cols, halo_cols)


def broadcast_from_owners(value, axes):
    count = 1
    for axis in axes:
        count *= lax.axis_size(axis)
    chunks = value.reshape(count, -1)
    own_chunk = lax.all_to_all(chunks, axes, 0, 0, tiled=True).sum(axis=0)
    spread = jnp.broadcast_to(own_chunk[None], chunks.shape)
    return lax.all_to_all(spread, axes, 0, 0, tiled=True).reshape(value.shape)


def neighbours(padded):
    return (padded[:, :-2, 1:-1], padded[:, 2:, 1:-1], padded[:, 1:-1, :-2], padded[:, 1:-1, 2:])


def face_terms(padded_perm):
    centre_perm = padded_perm[:, 1:-1, 1:-1]
    return [jnp.exp(0.5 * (centre_perm + near_perm)) for near_perm in neighbours(padded_perm)]


def advance(coefficients, bordered_head, source):
    centre_press = bordered_head[:, 1:-1, 1:-1]
    flux_total = jnp.zeros_like(centre_press)
    for weight_face, near_press in zip(coefficients, neighbours(bordered_head)):
        flux_total = flux_total + weight_face * (near_press - centre_press)
    return centre_press + time_step * (flux_total + source)


def blending_weights(predicted, observed, obs_var, perturb):
    member_count = predicted.shape[0]
    ensemble_spread = math.sqrt(member_count - 1)
    centred = (predicted - jnp.mean(predicted, axis=0, keepdims=True)) / ensemble_spread
    innovation = observed[None, :] + jnp.sqrt(obs_var)[None, :] * perturb - predicted
    weighted = centred / obs_var[None, :]
    system = jnp.eye(member_count, dtype=centred.dtype) + jnp.dot(
        weighted, centred.T, precision=lax.Precision.HIGHEST
    )
    right_side = jnp.dot(weighted, innovation.T, precision=lax.Precision.HIGHEST)
    factor = jnp.linalg.cholesky(system)
    half_solved = lax.linalg.triangular_solve(factor, right_side, left_side=True, lower=True)
    return lax.linalg.triangular_solve(
        factor, half_solved, left_side=True, lower=True, transpose_a=True
    )


def per_device(
    logarithmic_conductivity,
    starting_head,
    recharge,
    well_cells,
    well_owner,
    observed,
    obs_var,
    perturb,
):
    member_count, row_count, col_count = logarithmic_conductivity.shape
    width = STEPS
    ext_rows, ext_cols = row_count + 8, 2 * col_count
    f32 = jnp.float32

    def stack_rows(lo, hi):
        return jnp.concatenate(
            [logarithmic_conductivity[:, lo:hi], starting_head[:, lo:hi].astype(f32), recharge[None, lo:hi]], axis=0
        )

    top_rows = jnp.moveaxis(stack_rows(0, width), 1, 0)
    bottom_rows = jnp.moveaxis(stack_rows(row_count - width, row_count), 1, 0)
    from_above = jnp.moveaxis(send(bottom_rows, "row", True), 0, 1)
    from_below = jnp.moveaxis(send(top_rows, "row", False), 0, 1)
    stacked_total = from_above.shape[0]
    halo_rows = jnp.concatenate(
        [from_below, jnp.zeros((stacked_total, 8 - 2 * width, col_count), f32), from_above], axis=1
    )

    highest = lax.Precision.HIGHEST
    lane = jnp.arange(col_count)
    pick = jnp.arange(8)
    wanted = jnp.where(pick < width, pick, col_count - 8 + pick)
    selector = ((pick[:, None] < width) | (pick[:, None] >= 8 - width)) & (lane[None, :] == wanted[:, None])
    selector = selector.astype(f32)

    def columns(block):
        flat = block.reshape(-1, col_count)
        if block.dtype == jnp.bfloat16:
            return jnp.dot(selector.astype(jnp.bfloat16), flat.T, preferred_element_type=f32)
        return jnp.dot(selector, flat.T, precision=highest)

    interior_cols = jnp.concatenate(
        [
            columns(logarithmic_conductivity).reshape(8, member_count, row_count),
            columns(starting_head).reshape(8, member_count, row_count),
            columns(recharge).reshape(8, 1, row_count),
        ],
        axis=1,
    )
    border_cols = jnp.concatenate([interior_cols, columns(halo_rows).reshape(8, stacked_total, 8)], axis=2)
    from_left = send(border_cols[8 - width :], "col", True)
    from_right = send(border_cols[:width], "col", False)
    received = jnp.concatenate([from_right, jnp.zeros((8 - 2 * width,) + from_right.shape[1:], f32), from_left], axis=0)
    halo_cols = jnp.einsum("kmr,kl->mrl", received, selector, precision=highest)
    inside = circular_inside("row", row_count, width, ext_rows)[:, None] & circular_inside(
        "col", col_count, width, ext_cols
    )[None, :]
    pressure_low, hydraulic_head = run_stencil(
        inside.astype(f32), recharge, halo_rows, halo_cols, logarithmic_conductivity, starting_head, 8
    )
    group_total, well_count = well_cells.shape
    local_data = jnp.take(hydraulic_head.reshape(member_count, row_count * col_count), well_cells.reshape(-1), axis=1)
    me = lax.axis_index("row") * lax.axis_size("col") + lax.axis_index("col")
    mine = jnp.repeat(well_owner == me, well_count)
    local_data = jnp.where(mine[None, :], local_data, 0.0)
    predicted = broadcast_from_owners(local_data, ("row", "col"))
    mixing = blending_weights(predicted, observed, obs_var, perturb)
    ensemble_spread = math.sqrt(member_count - 1)
    anomalies = (
        logarithmic_conductivity - jnp.mean(logarithmic_conductivity, axis=0, keepdims=True)
    ) / ensemble_spread
    updated_perm = logarithmic_conductivity + jnp.einsum(
        "mrc,mn->nrc", anomalies, mixing, precision=lax.Precision.HIGHEST
    )
    return (pressure_low, predicted, updated_perm)


def solution(mesh):
    return jax.shard_map(
        per_device,
        mesh=mesh,
        in_specs=(
            P(None, "row", "col"),
            P(None, "row", "col"),
            P("row", "col"),
            P(),
            P(),
            P(),
            P(),
            P(),
        ),
        out_specs=(P(None, "row", "col"), P(), P(None, "row", "col")),
        check_vma=False,
    )
```

```python
import math

import jax
import jax.numpy as jnp
from jax import lax
from jax.sharding import PartitionSpec as P
from jax.experimental import pallas as pl
from jax.experimental.pallas import tpu as pltpu

STEPS = 3


time_step = 0.13


def send(piece, axis, forward):
    count = lax.axis_size(axis)
    pairs = [(i, i + 1) for i in range(count - 1)]
    if not forward:
        pairs = [(target, source) for source, target in pairs]
    return lax.ppermute(piece, axis, pairs)


def circular_inside(axis, local, width, size):
    index = jnp.arange(size)
    gap = (index >= local + width) & (index < size - width)
    local_index = jnp.where(index < local + width, index, index - size)
    global_index = lax.axis_index(axis) * local + local_index
    return (~gap) & (global_index >= 0) & (global_index < local * lax.axis_size(axis))


def stencil_kernel(mask_ref, source_ref, source_rows_ref, source_cols_ref, perm_ref, head_ref,
                   perm_rows_ref, head_rows_ref, perm_cols_ref, head_cols_ref, out16_ref, out32_ref):
    rows, cols = perm_ref.shape[1], perm_ref.shape[2]
    ext_rows, ext_cols = rows + 8, 2 * cols

    def extend(interior, halo_rows, halo_cols):
        return jnp.concatenate([jnp.concatenate([interior, halo_rows], axis=0), halo_cols], axis=1)

    inside = mask_ref[...] > 0.5
    source = extend(source_ref[...], source_rows_ref[0], source_cols_ref[0])

    def member(j, carry):
        perm = extend(perm_ref[j], perm_rows_ref[j], perm_cols_ref[j])
        head = extend(head_ref[j].astype(jnp.float32), head_rows_ref[j], head_cols_ref[j])
        vertical = jnp.exp(0.5 * (perm + pltpu.roll(perm, ext_rows - 1, 0)))
        horizontal = jnp.exp(0.5 * (perm + pltpu.roll(perm, ext_cols - 1, 1)))
        faces = (pltpu.roll(vertical, 1, 0), vertical, pltpu.roll(horizontal, 1, 1), horizontal)
        for step_index in range(STEPS):
            near = (pltpu.roll(head, 1, 0), pltpu.roll(head, ext_rows - 1, 0),
                    pltpu.roll(head, 1, 1), pltpu.roll(head, ext_cols - 1, 1))
            if step_index == STEPS - 1:
                crop = lambda x: x[:rows, :cols]
                near, weights, centre, src = [crop(x) for x in near], [crop(x) for x in faces], crop(head), crop(source)
            else:
                weights, centre, src = faces, head, source
            flux_total = jnp.zeros_like(centre)
            for weight_face, near_press in zip(weights, near):
                flux_total = flux_total + weight_face * (near_press - centre)
            head = centre + time_step * (flux_total + src)
            if step_index < STEPS - 1:
                head = jnp.where(inside, head, 0.0)
        final = head
        out32_ref[j] = final
        out16_ref[j] = final.astype(jnp.bfloat16)
        return carry

    lax.fori_loop(0, perm_ref.shape[0], member, 0, unroll=4)


def run_stencil(mask, source, halo_rows, halo_cols, perm, head, block):
    members, rows, cols = perm.shape
    blocks = members // block
    full2 = lambda shape: pl.BlockSpec(shape, lambda i: (0, 0))
    member_block = lambda shape, shift: pl.BlockSpec((block,) + shape, lambda i: (i + shift, 0, 0))
    last = lambda shape: pl.BlockSpec((1,) + shape, lambda i: (2 * members, 0, 0))
    ext_rows = rows + 8
    cells = members * ext_rows * 2 * cols
    return pl.pallas_call(
        stencil_kernel,
        grid=(blocks,),
        in_specs=[
            full2(mask.shape),
            full2(source.shape),
            last((8, cols)),
            last((ext_rows, cols)),
            member_block((rows, cols), 0),
            member_block((rows, cols), 0),
            member_block((8, cols), 0),
            member_block((8, cols), blocks),
            member_block((ext_rows, cols), 0),
            member_block((ext_rows, cols), blocks),
        ],
        out_specs=[member_block((rows, cols), 0), member_block((rows, cols), 0)],
        out_shape=[
            jax.ShapeDtypeStruct(perm.shape, jnp.bfloat16),
            jax.ShapeDtypeStruct(perm.shape, jnp.float32),
        ],
        cost_estimate=pl.CostEstimate(
            flops=cells * 80, transcendentals=cells * 2, bytes_accessed=members * rows * cols * 14
        ),
    )(mask, source, halo_rows, halo_cols, perm, head, halo_rows, halo_rows, halo_cols, halo_cols)


def broadcast_from_owners(value, axes):
    count = 1
    for axis in axes:
        count *= lax.axis_size(axis)
    chunks = value.reshape(count, -1)
    own_chunk = lax.all_to_all(chunks, axes, 0, 0, tiled=True).sum(axis=0)
    spread = jnp.broadcast_to(own_chunk[None], chunks.shape)
    return lax.all_to_all(spread, axes, 0, 0, tiled=True).reshape(value.shape)


def neighbours(padded):
    return (padded[:, :-2, 1:-1], padded[:, 2:, 1:-1], padded[:, 1:-1, :-2], padded[:, 1:-1, 2:])


def face_terms(padded_perm):
    centre_perm = padded_perm[:, 1:-1, 1:-1]
    return [jnp.exp(0.5 * (centre_perm + near_perm)) for near_perm in neighbours(padded_perm)]


def advance(coefficients, bordered_head, source):
    centre_press = bordered_head[:, 1:-1, 1:-1]
    flux_total = jnp.zeros_like(centre_press)
    for weight_face, near_press in zip(coefficients, neighbours(bordered_head)):
        flux_total = flux_total + weight_face * (near_press - centre_press)
    return centre_press + time_step * (flux_total + source)


def blending_weights(predicted, observed, obs_var, perturb):
    member_count = predicted.shape[0]
    ensemble_spread = math.sqrt(member_count - 1)
    centred = (predicted - jnp.mean(predicted, axis=0, keepdims=True)) / ensemble_spread
    innovation = observed[None, :] + jnp.sqrt(obs_var)[None, :] * perturb - predicted
    weighted = centred / obs_var[None, :]
    system = jnp.eye(member_count, dtype=centred.dtype) + jnp.dot(
        weighted, centred.T, precision=lax.Precision.HIGHEST
    )
    right_side = jnp.dot(weighted, innovation.T, precision=lax.Precision.HIGHEST)
    factor = jnp.linalg.cholesky(system)
    half_solved = lax.linalg.triangular_solve(factor, right_side, left_side=True, lower=True)
    return lax.linalg.triangular_solve(
        factor, half_solved, left_side=True, lower=True, transpose_a=True
    )


def per_device(
    logarithmic_conductivity,
    starting_head,
    recharge,
    well_cells,
    well_owner,
    observed,
    obs_var,
    perturb,
):
    member_count, row_count, col_count = logarithmic_conductivity.shape
    width = STEPS
    ext_rows, ext_cols = row_count + 8, 2 * col_count
    f32 = jnp.float32

    def stack_rows(lo, hi):
        return jnp.concatenate(
            [logarithmic_conductivity[:, lo:hi], starting_head[:, lo:hi].astype(f32), recharge[None, lo:hi]], axis=0
        )

    top_rows = jnp.moveaxis(stack_rows(0, width), 1, 0)
    bottom_rows = jnp.moveaxis(stack_rows(row_count - width, row_count), 1, 0)
    from_above = jnp.moveaxis(send(bottom_rows, "row", True), 0, 1)
    from_below = jnp.moveaxis(send(top_rows, "row", False), 0, 1)
    stacked_total = from_above.shape[0]
    halo_rows = jnp.concatenate(
        [from_below, jnp.zeros((stacked_total, 8 - 2 * width, col_count), f32), from_above], axis=1
    )

    highest = lax.Precision.HIGHEST
    lane = jnp.arange(col_count)
    pick = jnp.arange(8)
    wanted = jnp.where(pick < width, pick, col_count - 8 + pick)
    selector = ((pick[:, None] < width) | (pick[:, None] >= 8 - width)) & (lane[None, :] == wanted[:, None])
    selector = selector.astype(f32)

    def columns(block):
        flat = block.reshape(-1, col_count)
        if block.dtype == jnp.bfloat16:
            return jnp.dot(selector.astype(jnp.bfloat16), flat.T, preferred_element_type=f32)
        return jnp.dot(selector, flat.T, precision=highest)

    interior_cols = jnp.concatenate(
        [
            columns(logarithmic_conductivity).reshape(8, member_count, row_count),
            columns(starting_head).reshape(8, member_count, row_count),
            columns(recharge).reshape(8, 1, row_count),
        ],
        axis=1,
    )
    border_cols = jnp.concatenate([interior_cols, columns(halo_rows).reshape(8, stacked_total, 8)], axis=2)
    from_left = send(border_cols[8 - width :], "col", True)
    from_right = send(border_cols[:width], "col", False)
    received = jnp.concatenate([from_right, jnp.zeros((8 - 2 * width,) + from_right.shape[1:], f32), from_left], axis=0)
    halo_cols = jnp.einsum("kmr,kl->mrl", received, selector, precision=highest)
    inside = circular_inside("row", row_count, width, ext_rows)[:, None] & circular_inside(
        "col", col_count, width, ext_cols
    )[None, :]
    pressure_low, hydraulic_head = run_stencil(
        inside.astype(f32), recharge, halo_rows, halo_cols, logarithmic_conductivity, starting_head, 8
    )
    group_total, well_count = well_cells.shape
    local_data = jnp.take(hydraulic_head.reshape(member_count, row_count * col_count), well_cells.reshape(-1), axis=1)
    me = lax.axis_index("row") * lax.axis_size("col") + lax.axis_index("col")
    mine = jnp.repeat(well_owner == me, well_count)
    local_data = jnp.where(mine[None, :], local_data, 0.0)
    predicted = broadcast_from_owners(local_data, ("row", "col"))
    mixing = blending_weights(predicted, observed, obs_var, perturb)
    ensemble_spread = math.sqrt(member_count - 1)
    anomalies = (
        logarithmic_conductivity - jnp.mean(logarithmic_conductivity, axis=0, keepdims=True)
    ) / ensemble_spread
    updated_perm = logarithmic_conductivity + jnp.einsum(
        "mrc,mn->nrc", anomalies, mixing, precision=lax.Precision.HIGHEST
    )
    return (pressure_low, predicted, updated_perm)


def solution(mesh):
    return jax.shard_map(
        per_device,
        mesh=mesh,
        in_specs=(
            P(None, "row", "col"),
            P(None, "row", "col"),
            P("row", "col"),
            P(),
            P(),
            P(),
            P(),
            P(),
        ),
        out_specs=(P(None, "row", "col"), P(), P(None, "row", "col")),
        check_vma=False,
    )
```

```python
import math

import jax
import jax.numpy as jnp
from jax import lax
from jax.sharding import PartitionSpec as P
from jax.experimental import pallas as pl
from jax.experimental.pallas import tpu as pltpu

STEPS = 3


time_step = 0.13


def send(piece, axis, forward):
    count = lax.axis_size(axis)
    pairs = [(i, i + 1) for i in range(count - 1)]
    if not forward:
        pairs = [(target, source) for source, target in pairs]
    return lax.ppermute(piece, axis, pairs)


def circular_inside(axis, local, width, size):
    index = jnp.arange(size)
    gap = (index >= local + width) & (index < size - width)
    local_index = jnp.where(index < local + width, index, index - size)
    global_index = lax.axis_index(axis) * local + local_index
    return (~gap) & (global_index >= 0) & (global_index < local * lax.axis_size(axis))


def stencil_kernel(mask_ref, source_ref, source_rows_ref, source_cols_ref, perm_ref, head_ref,
                   perm_rows_ref, head_rows_ref, perm_cols_ref, head_cols_ref, out16_ref, out32_ref):
    rows, cols = perm_ref.shape[1], perm_ref.shape[2]
    ext_rows, ext_cols = rows + 8, 2 * cols

    def extend(interior, halo_rows, halo_cols):
        return jnp.concatenate([jnp.concatenate([interior, halo_rows], axis=0), halo_cols], axis=1)

    inside = mask_ref[...] > 0.5
    source = extend(source_ref[...], source_rows_ref[0], source_cols_ref[0])

    def member(j, carry):
        perm = extend(perm_ref[j], perm_rows_ref[j], perm_cols_ref[j])
        head = extend(head_ref[j].astype(jnp.float32), head_rows_ref[j], head_cols_ref[j])
        vertical = jnp.exp(0.5 * (perm + pltpu.roll(perm, ext_rows - 1, 0)))
        horizontal = jnp.exp(0.5 * (perm + pltpu.roll(perm, ext_cols - 1, 1)))
        faces = (pltpu.roll(vertical, 1, 0), vertical, pltpu.roll(horizontal, 1, 1), horizontal)
        for step_index in range(STEPS):
            near = (pltpu.roll(head, 1, 0), pltpu.roll(head, ext_rows - 1, 0),
                    pltpu.roll(head, 1, 1), pltpu.roll(head, ext_cols - 1, 1))
            if step_index == STEPS - 1:
                crop = lambda x: x[:rows, :cols]
                near, weights, centre, src = [crop(x) for x in near], [crop(x) for x in faces], crop(head), crop(source)
            else:
                weights, centre, src = faces, head, source
            flux_total = jnp.zeros_like(centre)
            for weight_face, near_press in zip(weights, near):
                flux_total = flux_total + weight_face * (near_press - centre)
            head = centre + time_step * (flux_total + src)
            if step_index < STEPS - 1:
                head = jnp.where(inside, head, 0.0)
        final = head
        out32_ref[j] = final
        out16_ref[j] = final.astype(jnp.bfloat16)
        return carry

    lax.fori_loop(0, perm_ref.shape[0], member, 0, unroll=2)


def run_stencil(mask, source, halo_rows, halo_cols, perm, head, block):
    members, rows, cols = perm.shape
    blocks = members // block
    full2 = lambda shape: pl.BlockSpec(shape, lambda i: (0, 0))
    member_block = lambda shape, shift: pl.BlockSpec((block,) + shape, lambda i: (i + shift, 0, 0))
    last = lambda shape: pl.BlockSpec((1,) + shape, lambda i: (2 * members, 0, 0))
    ext_rows = rows + 8
    cells = members * ext_rows * 2 * cols
    return pl.pallas_call(
        stencil_kernel,
        grid=(blocks,),
        in_specs=[
            full2(mask.shape),
            full2(source.shape),
            last((8, cols)),
            last((ext_rows, cols)),
            member_block((rows, cols), 0),
            member_block((rows, cols), 0),
            member_block((8, cols), 0),
            member_block((8, cols), blocks),
            member_block((ext_rows, cols), 0),
            member_block((ext_rows, cols), blocks),
        ],
        out_specs=[member_block((rows, cols), 0), member_block((rows, cols), 0)],
        out_shape=[
            jax.ShapeDtypeStruct(perm.shape, jnp.bfloat16),
            jax.ShapeDtypeStruct(perm.shape, jnp.float32),
        ],
        cost_estimate=pl.CostEstimate(
            flops=cells * 80, transcendentals=cells * 2, bytes_accessed=members * rows * cols * 14
        ),
    )(mask, source, halo_rows, halo_cols, perm, head, halo_rows, halo_rows, halo_cols, halo_cols)


def broadcast_from_owners(value, axes):
    count = 1
    for axis in axes:
        count *= lax.axis_size(axis)
    chunks = value.reshape(count, -1)
    own_chunk = lax.all_to_all(chunks, axes, 0, 0, tiled=True).sum(axis=0)
    spread = jnp.broadcast_to(own_chunk[None], chunks.shape)
    return lax.all_to_all(spread, axes, 0, 0, tiled=True).reshape(value.shape)


def neighbours(padded):
    return (padded[:, :-2, 1:-1], padded[:, 2:, 1:-1], padded[:, 1:-1, :-2], padded[:, 1:-1, 2:])


def face_terms(padded_perm):
    centre_perm = padded_perm[:, 1:-1, 1:-1]
    return [jnp.exp(0.5 * (centre_perm + near_perm)) for near_perm in neighbours(padded_perm)]


def advance(coefficients, bordered_head, source):
    centre_press = bordered_head[:, 1:-1, 1:-1]
    flux_total = jnp.zeros_like(centre_press)
    for weight_face, near_press in zip(coefficients, neighbours(bordered_head)):
        flux_total = flux_total + weight_face * (near_press - centre_press)
    return centre_press + time_step * (flux_total + source)


def blending_weights(predicted, observed, obs_var, perturb):
    member_count = predicted.shape[0]
    ensemble_spread = math.sqrt(member_count - 1)
    centred = (predicted - jnp.mean(predicted, axis=0, keepdims=True)) / ensemble_spread
    innovation = observed[None, :] + jnp.sqrt(obs_var)[None, :] * perturb - predicted
    weighted = centred / obs_var[None, :]
    system = jnp.eye(member_count, dtype=centred.dtype) + jnp.dot(
        weighted, centred.T, precision=lax.Precision.HIGHEST
    )
    right_side = jnp.dot(weighted, innovation.T, precision=lax.Precision.HIGHEST)
    factor = jnp.linalg.cholesky(system)
    half_solved = lax.linalg.triangular_solve(factor, right_side, left_side=True, lower=True)
    return lax.linalg.triangular_solve(
        factor, half_solved, left_side=True, lower=True, transpose_a=True
    )


def per_device(
    logarithmic_conductivity,
    starting_head,
    recharge,
    well_cells,
    well_owner,
    observed,
    obs_var,
    perturb,
):
    member_count, row_count, col_count = logarithmic_conductivity.shape
    width = STEPS
    ext_rows, ext_cols = row_count + 8, 2 * col_count
    f32 = jnp.float32

    def stack_rows(lo, hi):
        return jnp.concatenate(
            [logarithmic_conductivity[:, lo:hi], starting_head[:, lo:hi].astype(f32), recharge[None, lo:hi]], axis=0
        )

    top_rows = jnp.moveaxis(stack_rows(0, width), 1, 0)
    bottom_rows = jnp.moveaxis(stack_rows(row_count - width, row_count), 1, 0)
    from_above = jnp.moveaxis(send(bottom_rows, "row", True), 0, 1)
    from_below = jnp.moveaxis(send(top_rows, "row", False), 0, 1)
    stacked_total = from_above.shape[0]
    halo_rows = jnp.concatenate(
        [from_below, jnp.zeros((stacked_total, 8 - 2 * width, col_count), f32), from_above], axis=1
    )

    highest = lax.Precision.HIGHEST
    lane = jnp.arange(col_count)
    pick = jnp.arange(8)
    wanted = jnp.where(pick < width, pick, col_count - 8 + pick)
    selector = ((pick[:, None] < width) | (pick[:, None] >= 8 - width)) & (lane[None, :] == wanted[:, None])
    selector = selector.astype(f32)

    def columns(block):
        flat = block.reshape(-1, col_count)
        if block.dtype == jnp.bfloat16:
            return jnp.dot(selector.astype(jnp.bfloat16), flat.T, preferred_element_type=f32)
        return jnp.dot(selector, flat.T, precision=highest)

    interior_cols = jnp.concatenate(
        [
            columns(logarithmic_conductivity).reshape(8, member_count, row_count),
            columns(starting_head).reshape(8, member_count, row_count),
            columns(recharge).reshape(8, 1, row_count),
        ],
        axis=1,
    )
    border_cols = jnp.concatenate([interior_cols, columns(halo_rows).reshape(8, stacked_total, 8)], axis=2)
    from_left = send(border_cols[8 - width :], "col", True)
    from_right = send(border_cols[:width], "col", False)
    received = jnp.concatenate([from_right, jnp.zeros((8 - 2 * width,) + from_right.shape[1:], f32), from_left], axis=0)
    halo_cols = jnp.einsum("kmr,kl->mrl", received, selector, precision=highest)
    inside = circular_inside("row", row_count, width, ext_rows)[:, None] & circular_inside(
        "col", col_count, width, ext_cols
    )[None, :]
    pressure_low, hydraulic_head = run_stencil(
        inside.astype(f32), recharge, halo_rows, halo_cols, logarithmic_conductivity, starting_head, 16
    )
    group_total, well_count = well_cells.shape
    local_data = jnp.take(hydraulic_head.reshape(member_count, row_count * col_count), well_cells.reshape(-1), axis=1)
    me = lax.axis_index("row") * lax.axis_size("col") + lax.axis_index("col")
    mine = jnp.repeat(well_owner == me, well_count)
    local_data = jnp.where(mine[None, :], local_data, 0.0)
    predicted = broadcast_from_owners(local_data, ("row", "col"))
    mixing = blending_weights(predicted, observed, obs_var, perturb)
    ensemble_spread = math.sqrt(member_count - 1)
    anomalies = (
        logarithmic_conductivity - jnp.mean(logarithmic_conductivity, axis=0, keepdims=True)
    ) / ensemble_spread
    updated_perm = logarithmic_conductivity + jnp.einsum(
        "mrc,mn->nrc", anomalies, mixing, precision=lax.Precision.HIGHEST
    )
    return (pressure_low, predicted, updated_perm)


def solution(mesh):
    return jax.shard_map(
        per_device,
        mesh=mesh,
        in_specs=(
            P(None, "row", "col"),
            P(None, "row", "col"),
            P("row", "col"),
            P(),
            P(),
            P(),
            P(),
            P(),
        ),
        out_specs=(P(None, "row", "col"), P(), P(None, "row", "col")),
        check_vma=False,
    )
```

```python
import math

import jax
import jax.numpy as jnp
from jax import lax
from jax.sharding import PartitionSpec as P
from jax.experimental import pallas as pl
from jax.experimental.pallas import tpu as pltpu

STEPS = 3


time_step = 0.13


def send(piece, axis, forward):
    count = lax.axis_size(axis)
    pairs = [(i, i + 1) for i in range(count - 1)]
    if not forward:
        pairs = [(target, source) for source, target in pairs]
    return lax.ppermute(piece, axis, pairs)


def circular_inside(axis, local, width, size):
    index = jnp.arange(size)
    gap = (index >= local + width) & (index < size - width)
    local_index = jnp.where(index < local + width, index, index - size)
    global_index = lax.axis_index(axis) * local + local_index
    return (~gap) & (global_index >= 0) & (global_index < local * lax.axis_size(axis))


def stencil_kernel(mask_ref, source_ref, source_rows_ref, source_cols_ref, perm_ref, head_ref,
                   perm_rows_ref, head_rows_ref, perm_cols_ref, head_cols_ref, out16_ref, out32_ref):
    rows, cols = perm_ref.shape[1], perm_ref.shape[2]
    ext_rows, ext_cols = rows + 8, 2 * cols

    def extend(interior, halo_rows, halo_cols):
        return jnp.concatenate([jnp.concatenate([interior, halo_rows], axis=0), halo_cols], axis=1)

    inside = mask_ref[...] > 0.5
    source = extend(source_ref[...], source_rows_ref[0], source_cols_ref[0])

    def member(j, carry):
        perm = extend(perm_ref[j], perm_rows_ref[j], perm_cols_ref[j])
        head = extend(head_ref[j].astype(jnp.float32), head_rows_ref[j], head_cols_ref[j])
        vertical = jnp.exp(0.5 * (perm + pltpu.roll(perm, ext_rows - 1, 0)))
        horizontal = jnp.exp(0.5 * (perm + pltpu.roll(perm, ext_cols - 1, 1)))
        faces = (pltpu.roll(vertical, 1, 0), vertical, pltpu.roll(horizontal, 1, 1), horizontal)
        for step_index in range(STEPS):
            near = (pltpu.roll(head, 1, 0), pltpu.roll(head, ext_rows - 1, 0),
                    pltpu.roll(head, 1, 1), pltpu.roll(head, ext_cols - 1, 1))
            if step_index == STEPS - 1:
                crop = lambda x: x[:rows, :cols]
                near, weights, centre, src = [crop(x) for x in near], [crop(x) for x in faces], crop(head), crop(source)
            else:
                weights, centre, src = faces, head, source
            flux_total = jnp.zeros_like(centre)
            for weight_face, near_press in zip(weights, near):
                flux_total = flux_total + weight_face * (near_press - centre)
            head = centre + time_step * (flux_total + src)
            if step_index < STEPS - 1:
                head = jnp.where(inside, head, 0.0)
        final = head
        out32_ref[j] = final
        out16_ref[j] = final.astype(jnp.bfloat16)
        return carry

    lax.fori_loop(0, perm_ref.shape[0], member, 0, unroll=2)


def run_stencil(mask, source, halo_rows, halo_cols, perm, head, block):
    members, rows, cols = perm.shape
    blocks = members // block
    full2 = lambda shape: pl.BlockSpec(shape, lambda i: (0, 0))
    member_block = lambda shape, shift: pl.BlockSpec((block,) + shape, lambda i: (i + shift, 0, 0))
    last = lambda shape: pl.BlockSpec((1,) + shape, lambda i: (2 * members, 0, 0))
    ext_rows = rows + 8
    cells = members * ext_rows * 2 * cols
    return pl.pallas_call(
        stencil_kernel,
        grid=(blocks,),
        in_specs=[
            full2(mask.shape),
            full2(source.shape),
            last((8, cols)),
            last((ext_rows, cols)),
            member_block((rows, cols), 0),
            member_block((rows, cols), 0),
            member_block((8, cols), 0),
            member_block((8, cols), blocks),
            member_block((ext_rows, cols), 0),
            member_block((ext_rows, cols), blocks),
        ],
        out_specs=[member_block((rows, cols), 0), member_block((rows, cols), 0)],
        out_shape=[
            jax.ShapeDtypeStruct(perm.shape, jnp.bfloat16),
            jax.ShapeDtypeStruct(perm.shape, jnp.float32),
        ],
        cost_estimate=pl.CostEstimate(
            flops=cells * 80, transcendentals=cells * 2, bytes_accessed=members * rows * cols * 14
        ),
    )(mask, source, halo_rows, halo_cols, perm, head, halo_rows, halo_rows, halo_cols, halo_cols)


def broadcast_from_owners(value, axes):
    count = 1
    for axis in axes:
        count *= lax.axis_size(axis)
    chunks = value.reshape(count, -1)
    own_chunk = lax.all_to_all(chunks, axes, 0, 0, tiled=True).sum(axis=0)
    spread = jnp.broadcast_to(own_chunk[None], chunks.shape)
    return lax.all_to_all(spread, axes, 0, 0, tiled=True).reshape(value.shape)


def neighbours(padded):
    return (padded[:, :-2, 1:-1], padded[:, 2:, 1:-1], padded[:, 1:-1, :-2], padded[:, 1:-1, 2:])


def face_terms(padded_perm):
    centre_perm = padded_perm[:, 1:-1, 1:-1]
    return [jnp.exp(0.5 * (centre_perm + near_perm)) for near_perm in neighbours(padded_perm)]


def advance(coefficients, bordered_head, source):
    centre_press = bordered_head[:, 1:-1, 1:-1]
    flux_total = jnp.zeros_like(centre_press)
    for weight_face, near_press in zip(coefficients, neighbours(bordered_head)):
        flux_total = flux_total + weight_face * (near_press - centre_press)
    return centre_press + time_step * (flux_total + source)


def update_kernel(mix_t_ref, perm_ref, out_ref):
    members = mix_t_ref.shape[0]
    rows = perm_ref.shape[0] // members
    mix_t = mix_t_ref[...]
    spread = math.sqrt(members - 1)

    def body(r, carry):
        values = perm_ref[pl.ds(r, members, stride=rows)]
        anomalies = (values - jnp.mean(values, axis=0, keepdims=True)) / spread
        shift = jnp.dot(mix_t, anomalies, precision=lax.Precision.HIGHEST, preferred_element_type=jnp.float32)
        out_ref[pl.ds(r, members, stride=rows)] = values + shift
        return carry

    lax.fori_loop(0, rows, body, 0, unroll=8)


def run_update(perm, mixing):
    members, rows, cols = perm.shape
    flat = perm.reshape(members * rows, cols)
    out = pl.pallas_call(
        update_kernel,
        out_shape=jax.ShapeDtypeStruct(flat.shape, jnp.float32),
        cost_estimate=pl.CostEstimate(
            flops=2 * members * members * rows * cols, transcendentals=0, bytes_accessed=8 * members * rows * cols
        ),
    )(mixing.T, flat)
    return out.reshape(perm.shape)


def blending_weights(predicted, observed, obs_var, perturb):
    member_count = predicted.shape[0]
    ensemble_spread = math.sqrt(member_count - 1)
    centred = (predicted - jnp.mean(predicted, axis=0, keepdims=True)) / ensemble_spread
    innovation = observed[None, :] + jnp.sqrt(obs_var)[None, :] * perturb - predicted
    weighted = centred / obs_var[None, :]
    system = jnp.eye(member_count, dtype=centred.dtype) + jnp.dot(
        weighted, centred.T, precision=lax.Precision.HIGHEST
    )
    right_side = jnp.dot(weighted, innovation.T, precision=lax.Precision.HIGHEST)
    factor = jnp.linalg.cholesky(system)
    half_solved = lax.linalg.triangular_solve(factor, right_side, left_side=True, lower=True)
    return lax.linalg.triangular_solve(
        factor, half_solved, left_side=True, lower=True, transpose_a=True
    )


def per_device(
    logarithmic_conductivity,
    starting_head,
    recharge,
    well_cells,
    well_owner,
    observed,
    obs_var,
    perturb,
):
    member_count, row_count, col_count = logarithmic_conductivity.shape
    width = STEPS
    ext_rows, ext_cols = row_count + 8, 2 * col_count
    f32 = jnp.float32

    def stack_rows(lo, hi):
        return jnp.concatenate(
            [logarithmic_conductivity[:, lo:hi], starting_head[:, lo:hi].astype(f32), recharge[None, lo:hi]], axis=0
        )

    top_rows = jnp.moveaxis(stack_rows(0, width), 1, 0)
    bottom_rows = jnp.moveaxis(stack_rows(row_count - width, row_count), 1, 0)
    from_above = jnp.moveaxis(send(bottom_rows, "row", True), 0, 1)
    from_below = jnp.moveaxis(send(top_rows, "row", False), 0, 1)
    stacked_total = from_above.shape[0]
    halo_rows = jnp.concatenate(
        [from_below, jnp.zeros((stacked_total, 8 - 2 * width, col_count), f32), from_above], axis=1
    )

    highest = lax.Precision.HIGHEST
    lane = jnp.arange(col_count)
    pick = jnp.arange(8)
    wanted = jnp.where(pick < width, pick, col_count - 8 + pick)
    selector = ((pick[:, None] < width) | (pick[:, None] >= 8 - width)) & (lane[None, :] == wanted[:, None])
    selector = selector.astype(f32)

    def columns(block):
        flat = block.reshape(-1, col_count)
        if block.dtype == jnp.bfloat16:
            return jnp.dot(selector.astype(jnp.bfloat16), flat.T, preferred_element_type=f32)
        return jnp.dot(selector, flat.T, precision=highest)

    interior_cols = jnp.concatenate(
        [
            columns(logarithmic_conductivity).reshape(8, member_count, row_count),
            columns(starting_head).reshape(8, member_count, row_count),
            columns(recharge).reshape(8, 1, row_count),
        ],
        axis=1,
    )
    border_cols = jnp.concatenate([interior_cols, columns(halo_rows).reshape(8, stacked_total, 8)], axis=2)
    from_left = send(border_cols[8 - width :], "col", True)
    from_right = send(border_cols[:width], "col", False)
    received = jnp.concatenate([from_right, jnp.zeros((8 - 2 * width,) + from_right.shape[1:], f32), from_left], axis=0)
    halo_cols = jnp.einsum("kmr,kl->mrl", received, selector, precision=highest)
    inside = circular_inside("row", row_count, width, ext_rows)[:, None] & circular_inside(
        "col", col_count, width, ext_cols
    )[None, :]
    pressure_low, hydraulic_head = run_stencil(
        inside.astype(f32), recharge, halo_rows, halo_cols, logarithmic_conductivity, starting_head, 8
    )
    group_total, well_count = well_cells.shape
    local_data = jnp.take(hydraulic_head.reshape(member_count, row_count * col_count), well_cells.reshape(-1), axis=1)
    me = lax.axis_index("row") * lax.axis_size("col") + lax.axis_index("col")
    mine = jnp.repeat(well_owner == me, well_count)
    local_data = jnp.where(mine[None, :], local_data, 0.0)
    predicted = broadcast_from_owners(local_data, ("row", "col"))
    mixing = blending_weights(predicted, observed, obs_var, perturb)
    updated_perm = run_update(logarithmic_conductivity, mixing)
    return (pressure_low, predicted, updated_perm)


def solution(mesh):
    return jax.shard_map(
        per_device,
        mesh=mesh,
        in_specs=(
            P(None, "row", "col"),
            P(None, "row", "col"),
            P("row", "col"),
            P(),
            P(),
            P(),
            P(),
            P(),
        ),
        out_specs=(P(None, "row", "col"), P(), P(None, "row", "col")),
        check_vma=False,
    )
```

```python
import math

import jax
import jax.numpy as jnp
from jax import lax
from jax.sharding import PartitionSpec as P
from jax.experimental import pallas as pl
from jax.experimental.pallas import tpu as pltpu

STEPS = 3


time_step = 0.13


def send(piece, axis, forward):
    count = lax.axis_size(axis)
    pairs = [(i, i + 1) for i in range(count - 1)]
    if not forward:
        pairs = [(target, source) for source, target in pairs]
    return lax.ppermute(piece, axis, pairs)


def circular_inside(axis, local, width, size):
    index = jnp.arange(size)
    gap = (index >= local + width) & (index < size - width)
    local_index = jnp.where(index < local + width, index, index - size)
    global_index = lax.axis_index(axis) * local + local_index
    return (~gap) & (global_index >= 0) & (global_index < local * lax.axis_size(axis))


def stencil_kernel(mask_ref, source_ref, source_rows_ref, source_cols_ref, perm_ref, head_ref,
                   perm_rows_ref, head_rows_ref, perm_cols_ref, head_cols_ref, out16_ref, out32_ref):
    rows, cols = perm_ref.shape[1], perm_ref.shape[2]
    ext_rows, ext_cols = rows + 8, 2 * cols

    def extend(interior, halo_rows, halo_cols):
        return jnp.concatenate([jnp.concatenate([interior, halo_rows], axis=0), halo_cols], axis=1)

    inside = mask_ref[...] > 0.5
    source = extend(source_ref[...], source_rows_ref[0], source_cols_ref[0])

    def member(j, carry):
        perm = extend(perm_ref[j], perm_rows_ref[j], perm_cols_ref[j])
        head = extend(head_ref[j].astype(jnp.float32), head_rows_ref[j], head_cols_ref[j])
        vertical = jnp.exp(0.5 * (perm + pltpu.roll(perm, ext_rows - 1, 0)))
        horizontal = jnp.exp(0.5 * (perm + pltpu.roll(perm, ext_cols - 1, 1)))
        faces = (pltpu.roll(vertical, 1, 0), vertical, pltpu.roll(horizontal, 1, 1), horizontal)
        for step_index in range(STEPS):
            near = (pltpu.roll(head, 1, 0), pltpu.roll(head, ext_rows - 1, 0),
                    pltpu.roll(head, 1, 1), pltpu.roll(head, ext_cols - 1, 1))
            if step_index == STEPS - 1:
                crop = lambda x: x[:rows, :cols]
                near, weights, centre, src = [crop(x) for x in near], [crop(x) for x in faces], crop(head), crop(source)
            else:
                weights, centre, src = faces, head, source
            flux_total = jnp.zeros_like(centre)
            for weight_face, near_press in zip(weights, near):
                flux_total = flux_total + weight_face * (near_press - centre)
            head = centre + time_step * (flux_total + src)
            if step_index < STEPS - 1:
                head = jnp.where(inside, head, 0.0)
        final = head
        out32_ref[j] = final
        out16_ref[j] = final.astype(jnp.bfloat16)
        return carry

    lax.fori_loop(0, perm_ref.shape[0], member, 0, unroll=2)


def run_stencil(mask, source, halo_rows, halo_cols, perm, head, block):
    members, rows, cols = perm.shape
    blocks = members // block
    full2 = lambda shape: pl.BlockSpec(shape, lambda i: (0, 0))
    member_block = lambda shape, shift: pl.BlockSpec((block,) + shape, lambda i: (i + shift, 0, 0))
    last = lambda shape: pl.BlockSpec((1,) + shape, lambda i: (2 * members, 0, 0))
    ext_rows = rows + 8
    cells = members * ext_rows * 2 * cols
    return pl.pallas_call(
        stencil_kernel,
        grid=(blocks,),
        in_specs=[
            full2(mask.shape),
            full2(source.shape),
            last((8, cols)),
            last((ext_rows, cols)),
            member_block((rows, cols), 0),
            member_block((rows, cols), 0),
            member_block((8, cols), 0),
            member_block((8, cols), blocks),
            member_block((ext_rows, cols), 0),
            member_block((ext_rows, cols), blocks),
        ],
        out_specs=[member_block((rows, cols), 0), member_block((rows, cols), 0)],
        out_shape=[
            jax.ShapeDtypeStruct(perm.shape, jnp.bfloat16),
            jax.ShapeDtypeStruct(perm.shape, jnp.float32),
        ],
        cost_estimate=pl.CostEstimate(
            flops=cells * 80, transcendentals=cells * 2, bytes_accessed=members * rows * cols * 14
        ),
    )(mask, source, halo_rows, halo_cols, perm, head, halo_rows, halo_rows, halo_cols, halo_cols)


def broadcast_from_owners(value, axes):
    count = 1
    for axis in axes:
        count *= lax.axis_size(axis)
    chunks = value.reshape(count, -1)
    own_chunk = lax.all_to_all(chunks, axes, 0, 0, tiled=True).sum(axis=0)
    spread = jnp.broadcast_to(own_chunk[None], chunks.shape)
    return lax.all_to_all(spread, axes, 0, 0, tiled=True).reshape(value.shape)


def neighbours(padded):
    return (padded[:, :-2, 1:-1], padded[:, 2:, 1:-1], padded[:, 1:-1, :-2], padded[:, 1:-1, 2:])


def face_terms(padded_perm):
    centre_perm = padded_perm[:, 1:-1, 1:-1]
    return [jnp.exp(0.5 * (centre_perm + near_perm)) for near_perm in neighbours(padded_perm)]


def advance(coefficients, bordered_head, source):
    centre_press = bordered_head[:, 1:-1, 1:-1]
    flux_total = jnp.zeros_like(centre_press)
    for weight_face, near_press in zip(coefficients, neighbours(bordered_head)):
        flux_total = flux_total + weight_face * (near_press - centre_press)
    return centre_press + time_step * (flux_total + source)


def update_kernel(mix_t_ref, perm_ref, out_ref):
    members = mix_t_ref.shape[0]
    rows = perm_ref.shape[0] // members
    mix_t = mix_t_ref[...]
    spread = math.sqrt(members - 1)

    def body(r, carry):
        values = perm_ref[pl.ds(r, members, stride=rows)]
        anomalies = (values - jnp.mean(values, axis=0, keepdims=True)) / spread
        shift = jnp.dot(mix_t, anomalies, precision=lax.Precision.HIGHEST, preferred_element_type=jnp.float32)
        out_ref[pl.ds(r, members, stride=rows)] = values + shift
        return carry

    lax.fori_loop(0, rows, body, 0, unroll=16)


def run_update(perm, mixing):
    members, rows, cols = perm.shape
    flat = perm.reshape(members * rows, cols)
    out = pl.pallas_call(
        update_kernel,
        out_shape=jax.ShapeDtypeStruct(flat.shape, jnp.float32),
        cost_estimate=pl.CostEstimate(
            flops=2 * members * members * rows * cols, transcendentals=0, bytes_accessed=8 * members * rows * cols
        ),
    )(mixing.T, flat)
    return out.reshape(perm.shape)


def blending_weights(predicted, observed, obs_var, perturb):
    member_count = predicted.shape[0]
    ensemble_spread = math.sqrt(member_count - 1)
    centred = (predicted - jnp.mean(predicted, axis=0, keepdims=True)) / ensemble_spread
    innovation = observed[None, :] + jnp.sqrt(obs_var)[None, :] * perturb - predicted
    weighted = centred / obs_var[None, :]
    system = jnp.eye(member_count, dtype=centred.dtype) + jnp.dot(
        weighted, centred.T, precision=lax.Precision.HIGHEST
    )
    right_side = jnp.dot(weighted, innovation.T, precision=lax.Precision.HIGHEST)
    factor = jnp.linalg.cholesky(system)
    half_solved = lax.linalg.triangular_solve(factor, right_side, left_side=True, lower=True)
    return lax.linalg.triangular_solve(
        factor, half_solved, left_side=True, lower=True, transpose_a=True
    )


def per_device(
    logarithmic_conductivity,
    starting_head,
    recharge,
    well_cells,
    well_owner,
    observed,
    obs_var,
    perturb,
):
    member_count, row_count, col_count = logarithmic_conductivity.shape
    width = STEPS
    ext_rows, ext_cols = row_count + 8, 2 * col_count
    f32 = jnp.float32

    def stack_rows(lo, hi):
        return jnp.concatenate(
            [logarithmic_conductivity[:, lo:hi], starting_head[:, lo:hi].astype(f32), recharge[None, lo:hi]], axis=0
        )

    top_rows = jnp.moveaxis(stack_rows(0, width), 1, 0)
    bottom_rows = jnp.moveaxis(stack_rows(row_count - width, row_count), 1, 0)
    from_above = jnp.moveaxis(send(bottom_rows, "row", True), 0, 1)
    from_below = jnp.moveaxis(send(top_rows, "row", False), 0, 1)
    stacked_total = from_above.shape[0]
    halo_rows = jnp.concatenate(
        [from_below, jnp.zeros((stacked_total, 8 - 2 * width, col_count), f32), from_above], axis=1
    )

    highest = lax.Precision.HIGHEST
    lane = jnp.arange(col_count)
    pick = jnp.arange(8)
    wanted = jnp.where(pick < width, pick, col_count - 8 + pick)
    selector = ((pick[:, None] < width) | (pick[:, None] >= 8 - width)) & (lane[None, :] == wanted[:, None])
    selector = selector.astype(f32)

    def columns(block):
        flat = block.reshape(-1, col_count)
        if block.dtype == jnp.bfloat16:
            return jnp.dot(selector.astype(jnp.bfloat16), flat.T, preferred_element_type=f32)
        return jnp.dot(selector, flat.T, precision=highest)

    interior_cols = jnp.concatenate(
        [
            columns(logarithmic_conductivity).reshape(8, member_count, row_count),
            columns(starting_head).reshape(8, member_count, row_count),
            columns(recharge).reshape(8, 1, row_count),
        ],
        axis=1,
    )
    border_cols = jnp.concatenate([interior_cols, columns(halo_rows).reshape(8, stacked_total, 8)], axis=2)
    from_left = send(border_cols[8 - width :], "col", True)
    from_right = send(border_cols[:width], "col", False)
    received = jnp.concatenate([from_right, jnp.zeros((8 - 2 * width,) + from_right.shape[1:], f32), from_left], axis=0)
    halo_cols = jnp.einsum("kmr,kl->mrl", received, selector, precision=highest)
    inside = circular_inside("row", row_count, width, ext_rows)[:, None] & circular_inside(
        "col", col_count, width, ext_cols
    )[None, :]
    pressure_low, hydraulic_head = run_stencil(
        inside.astype(f32), recharge, halo_rows, halo_cols, logarithmic_conductivity, starting_head, 8
    )
    group_total, well_count = well_cells.shape
    local_data = jnp.take(hydraulic_head.reshape(member_count, row_count * col_count), well_cells.reshape(-1), axis=1)
    me = lax.axis_index("row") * lax.axis_size("col") + lax.axis_index("col")
    mine = jnp.repeat(well_owner == me, well_count)
    local_data = jnp.where(mine[None, :], local_data, 0.0)
    predicted = broadcast_from_owners(local_data, ("row", "col"))
    mixing = blending_weights(predicted, observed, obs_var, perturb)
    updated_perm = run_update(logarithmic_conductivity, mixing)
    return (pressure_low, predicted, updated_perm)


def solution(mesh):
    return jax.shard_map(
        per_device,
        mesh=mesh,
        in_specs=(
            P(None, "row", "col"),
            P(None, "row", "col"),
            P("row", "col"),
            P(),
            P(),
            P(),
            P(),
            P(),
        ),
        out_specs=(P(None, "row", "col"), P(), P(None, "row", "col")),
        check_vma=False,
    )
```

```python
import math

import jax
import jax.numpy as jnp
from jax import lax
from jax.sharding import PartitionSpec as P
from jax.experimental import pallas as pl
from jax.experimental.pallas import tpu as pltpu

STEPS = 3


time_step = 0.13


def send(piece, axis, forward):
    count = lax.axis_size(axis)
    pairs = [(i, i + 1) for i in range(count - 1)]
    if not forward:
        pairs = [(target, source) for source, target in pairs]
    return lax.ppermute(piece, axis, pairs)


def circular_inside(axis, local, width, size):
    index = jnp.arange(size)
    gap = (index >= local + width) & (index < size - width)
    local_index = jnp.where(index < local + width, index, index - size)
    global_index = lax.axis_index(axis) * local + local_index
    return (~gap) & (global_index >= 0) & (global_index < local * lax.axis_size(axis))


def stencil_kernel(mask_ref, source_ref, source_rows_ref, source_cols_ref, perm_ref, head_ref,
                   perm_rows_ref, head_rows_ref, perm_cols_ref, head_cols_ref, out16_ref, out32_ref):
    rows, cols = perm_ref.shape[1], perm_ref.shape[2]
    ext_rows, ext_cols = rows + 8, 2 * cols

    def extend(interior, halo_rows, halo_cols):
        return jnp.concatenate([jnp.concatenate([interior, halo_rows], axis=0), halo_cols], axis=1)

    inside = mask_ref[...] > 0.5
    source = extend(source_ref[...], source_rows_ref[0], source_cols_ref[0])

    def member(j, carry):
        perm = extend(perm_ref[j], perm_rows_ref[j], perm_cols_ref[j])
        head = extend(head_ref[j].astype(jnp.float32), head_rows_ref[j], head_cols_ref[j])
        vertical = jnp.exp(0.5 * (perm + pltpu.roll(perm, ext_rows - 1, 0)))
        horizontal = jnp.exp(0.5 * (perm + pltpu.roll(perm, ext_cols - 1, 1)))
        faces = (pltpu.roll(vertical, 1, 0), vertical, pltpu.roll(horizontal, 1, 1), horizontal)
        for step_index in range(STEPS):
            near = (pltpu.roll(head, 1, 0), pltpu.roll(head, ext_rows - 1, 0),
                    pltpu.roll(head, 1, 1), pltpu.roll(head, ext_cols - 1, 1))
            if step_index == STEPS - 1:
                crop = lambda x: x[:rows, :cols]
                near, weights, centre, src = [crop(x) for x in near], [crop(x) for x in faces], crop(head), crop(source)
            else:
                weights, centre, src = faces, head, source
            flux_total = jnp.zeros_like(centre)
            for weight_face, near_press in zip(weights, near):
                flux_total = flux_total + weight_face * (near_press - centre)
            head = centre + time_step * (flux_total + src)
            if step_index < STEPS - 1:
                head = jnp.where(inside, head, 0.0)
        final = head
        out32_ref[j] = final
        out16_ref[j] = final.astype(jnp.bfloat16)
        return carry

    lax.fori_loop(0, perm_ref.shape[0], member, 0, unroll=2)


def run_stencil(mask, source, halo_rows, halo_cols, perm, head, block):
    members, rows, cols = perm.shape
    blocks = members // block
    full2 = lambda shape: pl.BlockSpec(shape, lambda i: (0, 0))
    member_block = lambda shape, shift: pl.BlockSpec((block,) + shape, lambda i: (i + shift, 0, 0))
    last = lambda shape: pl.BlockSpec((1,) + shape, lambda i: (2 * members, 0, 0))
    ext_rows = rows + 8
    cells = members * ext_rows * 2 * cols
    return pl.pallas_call(
        stencil_kernel,
        grid=(blocks,),
        in_specs=[
            full2(mask.shape),
            full2(source.shape),
            last((8, cols)),
            last((ext_rows, cols)),
            member_block((rows, cols), 0),
            member_block((rows, cols), 0),
            member_block((8, cols), 0),
            member_block((8, cols), blocks),
            member_block((ext_rows, cols), 0),
            member_block((ext_rows, cols), blocks),
        ],
        out_specs=[member_block((rows, cols), 0), member_block((rows, cols), 0)],
        out_shape=[
            jax.ShapeDtypeStruct(perm.shape, jnp.bfloat16),
            jax.ShapeDtypeStruct(perm.shape, jnp.float32),
        ],
        cost_estimate=pl.CostEstimate(
            flops=cells * 80, transcendentals=cells * 2, bytes_accessed=members * rows * cols * 14
        ),
    )(mask, source, halo_rows, halo_cols, perm, head, halo_rows, halo_rows, halo_cols, halo_cols)


def broadcast_from_owners(value, axes):
    count = 1
    for axis in axes:
        count *= lax.axis_size(axis)
    chunks = value.reshape(count, -1)
    own_chunk = lax.all_to_all(chunks, axes, 0, 0, tiled=True).sum(axis=0)
    spread = jnp.broadcast_to(own_chunk[None], chunks.shape)
    return lax.all_to_all(spread, axes, 0, 0, tiled=True).reshape(value.shape)


def neighbours(padded):
    return (padded[:, :-2, 1:-1], padded[:, 2:, 1:-1], padded[:, 1:-1, :-2], padded[:, 1:-1, 2:])


def face_terms(padded_perm):
    centre_perm = padded_perm[:, 1:-1, 1:-1]
    return [jnp.exp(0.5 * (centre_perm + near_perm)) for near_perm in neighbours(padded_perm)]


def advance(coefficients, bordered_head, source):
    centre_press = bordered_head[:, 1:-1, 1:-1]
    flux_total = jnp.zeros_like(centre_press)
    for weight_face, near_press in zip(coefficients, neighbours(bordered_head)):
        flux_total = flux_total + weight_face * (near_press - centre_press)
    return centre_press + time_step * (flux_total + source)


def update_kernel(mix_t_ref, perm_ref, anomaly_ref, out_ref):
    members = mix_t_ref.shape[0]
    rows = perm_ref.shape[0] // members
    mix_t = mix_t_ref[...]

    def body(r, carry):
        window = pl.ds(r, members, stride=rows)
        shift = jnp.dot(mix_t, anomaly_ref[window], precision=lax.Precision.HIGHEST, preferred_element_type=jnp.float32)
        out_ref[window] = perm_ref[window] + shift
        return carry

    lax.fori_loop(0, rows, body, 0, unroll=8)


def run_update(perm, mixing):
    members, rows, cols = perm.shape
    anomalies = (perm - jnp.mean(perm, axis=0, keepdims=True)) / math.sqrt(members - 1)
    flat = perm.reshape(members * rows, cols)
    out = pl.pallas_call(
        update_kernel,
        out_shape=jax.ShapeDtypeStruct(flat.shape, jnp.float32),
        cost_estimate=pl.CostEstimate(
            flops=2 * members * members * rows * cols, transcendentals=0, bytes_accessed=12 * members * rows * cols
        ),
    )(mixing.T, flat, anomalies.reshape(flat.shape))
    return out.reshape(perm.shape)


def blending_weights(predicted, observed, obs_var, perturb):
    member_count = predicted.shape[0]
    ensemble_spread = math.sqrt(member_count - 1)
    centred = (predicted - jnp.mean(predicted, axis=0, keepdims=True)) / ensemble_spread
    innovation = observed[None, :] + jnp.sqrt(obs_var)[None, :] * perturb - predicted
    weighted = centred / obs_var[None, :]
    system = jnp.eye(member_count, dtype=centred.dtype) + jnp.dot(
        weighted, centred.T, precision=lax.Precision.HIGHEST
    )
    right_side = jnp.dot(weighted, innovation.T, precision=lax.Precision.HIGHEST)
    factor = jnp.linalg.cholesky(system)
    half_solved = lax.linalg.triangular_solve(factor, right_side, left_side=True, lower=True)
    return lax.linalg.triangular_solve(
        factor, half_solved, left_side=True, lower=True, transpose_a=True
    )


def per_device(
    logarithmic_conductivity,
    starting_head,
    recharge,
    well_cells,
    well_owner,
    observed,
    obs_var,
    perturb,
):
    member_count, row_count, col_count = logarithmic_conductivity.shape
    width = STEPS
    ext_rows, ext_cols = row_count + 8, 2 * col_count
    f32 = jnp.float32

    def stack_rows(lo, hi):
        return jnp.concatenate(
            [logarithmic_conductivity[:, lo:hi], starting_head[:, lo:hi].astype(f32), recharge[None, lo:hi]], axis=0
        )

    top_rows = jnp.moveaxis(stack_rows(0, width), 1, 0)
    bottom_rows = jnp.moveaxis(stack_rows(row_count - width, row_count), 1, 0)
    from_above = jnp.moveaxis(send(bottom_rows, "row", True), 0, 1)
    from_below = jnp.moveaxis(send(top_rows, "row", False), 0, 1)
    stacked_total = from_above.shape[0]
    halo_rows = jnp.concatenate(
        [from_below, jnp.zeros((stacked_total, 8 - 2 * width, col_count), f32), from_above], axis=1
    )

    highest = lax.Precision.HIGHEST
    lane = jnp.arange(col_count)
    pick = jnp.arange(8)
    wanted = jnp.where(pick < width, pick, col_count - 8 + pick)
    selector = ((pick[:, None] < width) | (pick[:, None] >= 8 - width)) & (lane[None, :] == wanted[:, None])
    selector = selector.astype(f32)

    def columns(block):
        flat = block.reshape(-1, col_count)
        if block.dtype == jnp.bfloat16:
            return jnp.dot(selector.astype(jnp.bfloat16), flat.T, preferred_element_type=f32)
        return jnp.dot(selector, flat.T, precision=highest)

    interior_cols = jnp.concatenate(
        [
            columns(logarithmic_conductivity).reshape(8, member_count, row_count),
            columns(starting_head).reshape(8, member_count, row_count),
            columns(recharge).reshape(8, 1, row_count),
        ],
        axis=1,
    )
    border_cols = jnp.concatenate([interior_cols, columns(halo_rows).reshape(8, stacked_total, 8)], axis=2)
    from_left = send(border_cols[8 - width :], "col", True)
    from_right = send(border_cols[:width], "col", False)
    received = jnp.concatenate([from_right, jnp.zeros((8 - 2 * width,) + from_right.shape[1:], f32), from_left], axis=0)
    halo_cols = jnp.einsum("kmr,kl->mrl", received, selector, precision=highest)
    inside = circular_inside("row", row_count, width, ext_rows)[:, None] & circular_inside(
        "col", col_count, width, ext_cols
    )[None, :]
    pressure_low, hydraulic_head = run_stencil(
        inside.astype(f32), recharge, halo_rows, halo_cols, logarithmic_conductivity, starting_head, 8
    )
    group_total, well_count = well_cells.shape
    local_data = jnp.take(hydraulic_head.reshape(member_count, row_count * col_count), well_cells.reshape(-1), axis=1)
    me = lax.axis_index("row") * lax.axis_size("col") + lax.axis_index("col")
    mine = jnp.repeat(well_owner == me, well_count)
    local_data = jnp.where(mine[None, :], local_data, 0.0)
    predicted = broadcast_from_owners(local_data, ("row", "col"))
    mixing = blending_weights(predicted, observed, obs_var, perturb)
    updated_perm = run_update(logarithmic_conductivity, mixing)
    return (pressure_low, predicted, updated_perm)


def solution(mesh):
    return jax.shard_map(
        per_device,
        mesh=mesh,
        in_specs=(
            P(None, "row", "col"),
            P(None, "row", "col"),
            P("row", "col"),
            P(),
            P(),
            P(),
            P(),
            P(),
        ),
        out_specs=(P(None, "row", "col"), P(), P(None, "row", "col")),
        check_vma=False,
    )
```

```python
import math

import jax
import jax.numpy as jnp
from jax import lax
from jax.sharding import PartitionSpec as P
from jax.experimental import pallas as pl
from jax.experimental.pallas import tpu as pltpu

STEPS = 3


time_step = 0.13


def send(piece, axis, forward):
    count = lax.axis_size(axis)
    pairs = [(i, i + 1) for i in range(count - 1)]
    if not forward:
        pairs = [(target, source) for source, target in pairs]
    return lax.ppermute(piece, axis, pairs)


def circular_inside(axis, local, width, size):
    index = jnp.arange(size)
    gap = (index >= local + width) & (index < size - width)
    local_index = jnp.where(index < local + width, index, index - size)
    global_index = lax.axis_index(axis) * local + local_index
    return (~gap) & (global_index >= 0) & (global_index < local * lax.axis_size(axis))


def stencil_kernel(mask_ref, source_ref, source_rows_ref, source_cols_ref, perm_ref, head_ref,
                   perm_rows_ref, head_rows_ref, perm_cols_ref, head_cols_ref, out16_ref, out32_ref):
    rows, cols = perm_ref.shape[1], perm_ref.shape[2]
    ext_rows, ext_cols = rows + 8, 2 * cols

    def extend(interior, halo_rows, halo_cols):
        return jnp.concatenate([jnp.concatenate([interior, halo_rows], axis=0), halo_cols], axis=1)

    inside = mask_ref[...] > 0.5
    source = extend(source_ref[...], source_rows_ref[0], source_cols_ref[0])

    def member(j, carry):
        perm = extend(perm_ref[j], perm_rows_ref[j], perm_cols_ref[j])
        head = extend(head_ref[j].astype(jnp.float32), head_rows_ref[j], head_cols_ref[j])
        vertical = jnp.exp(0.5 * (perm + pltpu.roll(perm, ext_rows - 1, 0)))
        horizontal = jnp.exp(0.5 * (perm + pltpu.roll(perm, ext_cols - 1, 1)))
        faces = (pltpu.roll(vertical, 1, 0), vertical, pltpu.roll(horizontal, 1, 1), horizontal)
        for step_index in range(STEPS):
            near = (pltpu.roll(head, 1, 0), pltpu.roll(head, ext_rows - 1, 0),
                    pltpu.roll(head, 1, 1), pltpu.roll(head, ext_cols - 1, 1))
            if step_index == STEPS - 1:
                crop = lambda x: x[:rows, :cols]
                near, weights, centre, src = [crop(x) for x in near], [crop(x) for x in faces], crop(head), crop(source)
            else:
                weights, centre, src = faces, head, source
            flux_total = jnp.zeros_like(centre)
            for weight_face, near_press in zip(weights, near):
                flux_total = flux_total + weight_face * (near_press - centre)
            head = centre + time_step * (flux_total + src)
            if step_index < STEPS - 1:
                head = jnp.where(inside, head, 0.0)
        final = head
        out32_ref[j] = final
        out16_ref[j] = final.astype(jnp.bfloat16)
        return carry

    lax.fori_loop(0, perm_ref.shape[0], member, 0, unroll=2)


def run_stencil(mask, source, halo_rows, halo_cols, perm, head, block):
    members, rows, cols = perm.shape
    blocks = members // block
    full2 = lambda shape: pl.BlockSpec(shape, lambda i: (0, 0))
    member_block = lambda shape, shift: pl.BlockSpec((block,) + shape, lambda i: (i + shift, 0, 0))
    last = lambda shape: pl.BlockSpec((1,) + shape, lambda i: (2 * members, 0, 0))
    ext_rows = rows + 8
    cells = members * ext_rows * 2 * cols
    return pl.pallas_call(
        stencil_kernel,
        grid=(blocks,),
        in_specs=[
            full2(mask.shape),
            full2(source.shape),
            last((8, cols)),
            last((ext_rows, cols)),
            member_block((rows, cols), 0),
            member_block((rows, cols), 0),
            member_block((8, cols), 0),
            member_block((8, cols), blocks),
            member_block((ext_rows, cols), 0),
            member_block((ext_rows, cols), blocks),
        ],
        out_specs=[member_block((rows, cols), 0), member_block((rows, cols), 0)],
        out_shape=[
            jax.ShapeDtypeStruct(perm.shape, jnp.bfloat16),
            jax.ShapeDtypeStruct(perm.shape, jnp.float32),
        ],
        cost_estimate=pl.CostEstimate(
            flops=cells * 80, transcendentals=cells * 2, bytes_accessed=members * rows * cols * 14
        ),
    )(mask, source, halo_rows, halo_cols, perm, head, halo_rows, halo_rows, halo_cols, halo_cols)


def broadcast_from_owners(value, axes):
    count = 1
    for axis in axes:
        count *= lax.axis_size(axis)
    chunks = value.reshape(count, -1)
    own_chunk = lax.all_to_all(chunks, axes, 0, 0, tiled=True).sum(axis=0)
    spread = jnp.broadcast_to(own_chunk[None], chunks.shape)
    return lax.all_to_all(spread, axes, 0, 0, tiled=True).reshape(value.shape)


def neighbours(padded):
    return (padded[:, :-2, 1:-1], padded[:, 2:, 1:-1], padded[:, 1:-1, :-2], padded[:, 1:-1, 2:])


def face_terms(padded_perm):
    centre_perm = padded_perm[:, 1:-1, 1:-1]
    return [jnp.exp(0.5 * (centre_perm + near_perm)) for near_perm in neighbours(padded_perm)]


def advance(coefficients, bordered_head, source):
    centre_press = bordered_head[:, 1:-1, 1:-1]
    flux_total = jnp.zeros_like(centre_press)
    for weight_face, near_press in zip(coefficients, neighbours(bordered_head)):
        flux_total = flux_total + weight_face * (near_press - centre_press)
    return centre_press + time_step * (flux_total + source)


def update_kernel(mix_t_ref, perm_ref, out_ref):
    members = mix_t_ref.shape[0]
    rows = perm_ref.shape[0] // members
    mix_t = mix_t_ref[...]
    spread = math.sqrt(members - 1)

    def body(r, carry):
        values = perm_ref[pl.ds(r, members, stride=rows)]
        anomalies = (values - jnp.mean(values, axis=0, keepdims=True)) / spread
        shift = jnp.dot(mix_t, anomalies, precision=lax.Precision.HIGHEST, preferred_element_type=jnp.float32)
        out_ref[pl.ds(r, members, stride=rows)] = values + shift
        return carry

    lax.fori_loop(0, rows, body, 0, unroll=8)


def run_update(perm, mixing):
    members, rows, cols = perm.shape
    flat = perm.reshape(members * rows, cols)
    out = pl.pallas_call(
        update_kernel,
        out_shape=jax.ShapeDtypeStruct(flat.shape, jnp.float32),
        cost_estimate=pl.CostEstimate(
            flops=2 * members * members * rows * cols, transcendentals=0, bytes_accessed=8 * members * rows * cols
        ),
    )(mixing.T, flat)
    return out.reshape(perm.shape)


def blending_weights(predicted, observed, obs_var, perturb):
    member_count = predicted.shape[0]
    ensemble_spread = math.sqrt(member_count - 1)
    centred = (predicted - jnp.mean(predicted, axis=0, keepdims=True)) / ensemble_spread
    innovation = observed[None, :] + jnp.sqrt(obs_var)[None, :] * perturb - predicted
    weighted = centred / obs_var[None, :]
    system = jnp.eye(member_count, dtype=centred.dtype) + jnp.dot(
        weighted, centred.T, precision=lax.Precision.HIGHEST
    )
    right_side = jnp.dot(weighted, innovation.T, precision=lax.Precision.HIGHEST)
    factor = jnp.linalg.cholesky(system)
    half_solved = lax.linalg.triangular_solve(factor, right_side, left_side=True, lower=True)
    return lax.linalg.triangular_solve(
        factor, half_solved, left_side=True, lower=True, transpose_a=True
    )


def per_device(
    logarithmic_conductivity,
    starting_head,
    recharge,
    well_cells,
    well_owner,
    observed,
    obs_var,
    perturb,
):
    member_count, row_count, col_count = logarithmic_conductivity.shape
    width = STEPS
    ext_rows, ext_cols = row_count + 8, 2 * col_count
    f32 = jnp.float32

    def stack_rows(lo, hi):
        return jnp.concatenate(
            [logarithmic_conductivity[:, lo:hi], starting_head[:, lo:hi].astype(f32), recharge[None, lo:hi]], axis=0
        )

    top_rows = jnp.moveaxis(stack_rows(0, width), 1, 0)
    bottom_rows = jnp.moveaxis(stack_rows(row_count - width, row_count), 1, 0)
    from_above = jnp.moveaxis(send(bottom_rows, "row", True), 0, 1)
    from_below = jnp.moveaxis(send(top_rows, "row", False), 0, 1)
    stacked_total = from_above.shape[0]
    halo_rows = jnp.concatenate(
        [from_below, jnp.zeros((stacked_total, 8 - 2 * width, col_count), f32), from_above], axis=1
    )

    highest = lax.Precision.HIGHEST
    lane = jnp.arange(col_count)
    pick = jnp.arange(8)
    wanted = jnp.where(pick < width, pick, col_count - 8 + pick)
    selector = ((pick[:, None] < width) | (pick[:, None] >= 8 - width)) & (lane[None, :] == wanted[:, None])
    selector = selector.astype(f32)

    def columns(block):
        flat = block.reshape(-1, col_count)
        if block.dtype == jnp.bfloat16:
            return jnp.dot(selector.astype(jnp.bfloat16), flat.T, preferred_element_type=f32)
        return jnp.dot(selector, flat.T, precision=highest)

    interior_cols = jnp.concatenate(
        [
            columns(logarithmic_conductivity).reshape(8, member_count, row_count),
            columns(starting_head).reshape(8, member_count, row_count),
            columns(recharge).reshape(8, 1, row_count),
        ],
        axis=1,
    )
    border_cols = jnp.concatenate([interior_cols, columns(halo_rows).reshape(8, stacked_total, 8)], axis=2)
    from_left = send(border_cols[8 - width :], "col", True)
    from_right = send(border_cols[:width], "col", False)
    received = jnp.concatenate([from_right, jnp.zeros((8 - 2 * width,) + from_right.shape[1:], f32), from_left], axis=0)
    halo_cols = jnp.einsum("kmr,kl->mrl", received, selector, precision=highest)
    inside = circular_inside("row", row_count, width, ext_rows)[:, None] & circular_inside(
        "col", col_count, width, ext_cols
    )[None, :]
    pressure_low, hydraulic_head = run_stencil(
        inside.astype(f32), recharge, halo_rows, halo_cols, logarithmic_conductivity, starting_head, 4
    )
    group_total, well_count = well_cells.shape
    local_data = jnp.take(hydraulic_head.reshape(member_count, row_count * col_count), well_cells.reshape(-1), axis=1)
    me = lax.axis_index("row") * lax.axis_size("col") + lax.axis_index("col")
    mine = jnp.repeat(well_owner == me, well_count)
    local_data = jnp.where(mine[None, :], local_data, 0.0)
    predicted = broadcast_from_owners(local_data, ("row", "col"))
    mixing = blending_weights(predicted, observed, obs_var, perturb)
    updated_perm = run_update(logarithmic_conductivity, mixing)
    return (pressure_low, predicted, updated_perm)


def solution(mesh):
    return jax.shard_map(
        per_device,
        mesh=mesh,
        in_specs=(
            P(None, "row", "col"),
            P(None, "row", "col"),
            P("row", "col"),
            P(),
            P(),
            P(),
            P(),
            P(),
        ),
        out_specs=(P(None, "row", "col"), P(), P(None, "row", "col")),
        check_vma=False,
    )
```

```python
import math

import jax
import jax.numpy as jnp
from jax import lax
from jax.sharding import PartitionSpec as P
from jax.experimental import pallas as pl
from jax.experimental.pallas import tpu as pltpu

STEPS = 3


time_step = 0.13


def send(piece, axis, forward):
    count = lax.axis_size(axis)
    pairs = [(i, i + 1) for i in range(count - 1)]
    if not forward:
        pairs = [(target, source) for source, target in pairs]
    return lax.ppermute(piece, axis, pairs)


def circular_inside(axis, local, width, size):
    index = jnp.arange(size)
    gap = (index >= local + width) & (index < size - width)
    local_index = jnp.where(index < local + width, index, index - size)
    global_index = lax.axis_index(axis) * local + local_index
    return (~gap) & (global_index >= 0) & (global_index < local * lax.axis_size(axis))


def stencil_kernel(mask_ref, source_ref, source_rows_ref, source_cols_ref, perm_ref, head_ref,
                   perm_rows_ref, head_rows_ref, perm_cols_ref, head_cols_ref, out16_ref, out32_ref):
    rows, cols = perm_ref.shape[1], perm_ref.shape[2]
    ext_rows, ext_cols = rows + 8, 2 * cols

    def extend(interior, halo_rows, halo_cols):
        return jnp.concatenate([jnp.concatenate([interior, halo_rows], axis=0), halo_cols], axis=1)

    inside = mask_ref[...] > 0.5
    source = extend(source_ref[...], source_rows_ref[0], source_cols_ref[0])

    def member(j, carry):
        perm = extend(perm_ref[j], perm_rows_ref[j], perm_cols_ref[j])
        head = extend(head_ref[j].astype(jnp.float32), head_rows_ref[j], head_cols_ref[j])
        vertical = jnp.exp(0.5 * (perm + pltpu.roll(perm, ext_rows - 1, 0)))
        horizontal = jnp.exp(0.5 * (perm + pltpu.roll(perm, ext_cols - 1, 1)))
        faces = (pltpu.roll(vertical, 1, 0), vertical, pltpu.roll(horizontal, 1, 1), horizontal)
        for step_index in range(STEPS):
            near = (pltpu.roll(head, 1, 0), pltpu.roll(head, ext_rows - 1, 0),
                    pltpu.roll(head, 1, 1), pltpu.roll(head, ext_cols - 1, 1))
            if step_index == STEPS - 1:
                crop = lambda x: x[:rows, :cols]
                near, weights, centre, src = [crop(x) for x in near], [crop(x) for x in faces], crop(head), crop(source)
            else:
                weights, centre, src = faces, head, source
            flux_total = jnp.zeros_like(centre)
            for weight_face, near_press in zip(weights, near):
                flux_total = flux_total + weight_face * (near_press - centre)
            head = centre + time_step * (flux_total + src)
            if step_index < STEPS - 1:
                head = jnp.where(inside, head, 0.0)
        final = head
        out32_ref[j] = final
        out16_ref[j] = final.astype(jnp.bfloat16)
        return carry

    lax.fori_loop(0, perm_ref.shape[0], member, 0, unroll=2)


def run_stencil(mask, source, halo_rows, halo_cols, perm, head, block):
    members, rows, cols = perm.shape
    blocks = members // block
    full2 = lambda shape: pl.BlockSpec(shape, lambda i: (0, 0))
    member_block = lambda shape, shift: pl.BlockSpec((block,) + shape, lambda i: (i + shift, 0, 0))
    last = lambda shape: pl.BlockSpec((1,) + shape, lambda i: (2 * members, 0, 0))
    ext_rows = rows + 8
    cells = members * ext_rows * 2 * cols
    return pl.pallas_call(
        stencil_kernel,
        grid=(blocks,),
        in_specs=[
            full2(mask.shape),
            full2(source.shape),
            last((8, cols)),
            last((ext_rows, cols)),
            member_block((rows, cols), 0),
            member_block((rows, cols), 0),
            member_block((8, cols), 0),
            member_block((8, cols), blocks),
            member_block((ext_rows, cols), 0),
            member_block((ext_rows, cols), blocks),
        ],
        out_specs=[member_block((rows, cols), 0), member_block((rows, cols), 0)],
        out_shape=[
            jax.ShapeDtypeStruct(perm.shape, jnp.bfloat16),
            jax.ShapeDtypeStruct(perm.shape, jnp.float32),
        ],
        cost_estimate=pl.CostEstimate(
            flops=cells * 80, transcendentals=cells * 2, bytes_accessed=members * rows * cols * 14
        ),
    )(mask, source, halo_rows, halo_cols, perm, head, halo_rows, halo_rows, halo_cols, halo_cols)


def broadcast_from_owners(value, axes):
    count = 1
    for axis in axes:
        count *= lax.axis_size(axis)
    chunks = value.reshape(count, -1)
    own_chunk = lax.all_to_all(chunks, axes, 0, 0, tiled=True).sum(axis=0)
    spread = jnp.broadcast_to(own_chunk[None], chunks.shape)
    return lax.all_to_all(spread, axes, 0, 0, tiled=True).reshape(value.shape)


def neighbours(padded):
    return (padded[:, :-2, 1:-1], padded[:, 2:, 1:-1], padded[:, 1:-1, :-2], padded[:, 1:-1, 2:])


def face_terms(padded_perm):
    centre_perm = padded_perm[:, 1:-1, 1:-1]
    return [jnp.exp(0.5 * (centre_perm + near_perm)) for near_perm in neighbours(padded_perm)]


def advance(coefficients, bordered_head, source):
    centre_press = bordered_head[:, 1:-1, 1:-1]
    flux_total = jnp.zeros_like(centre_press)
    for weight_face, near_press in zip(coefficients, neighbours(bordered_head)):
        flux_total = flux_total + weight_face * (near_press - centre_press)
    return centre_press + time_step * (flux_total + source)


def update_kernel(mix_t_ref, perm_ref, out_ref):
    members = mix_t_ref.shape[0]
    rows = perm_ref.shape[0] // members
    mix_t = mix_t_ref[...]
    spread = math.sqrt(members - 1)

    def body(r, carry):
        values = perm_ref[pl.ds(r, members, stride=rows)]
        anomalies = (values - jnp.mean(values, axis=0, keepdims=True)) / spread
        shift = jnp.dot(mix_t, anomalies, precision=lax.Precision.HIGHEST, preferred_element_type=jnp.float32)
        out_ref[pl.ds(r, members, stride=rows)] = values + shift
        return carry

    lax.fori_loop(0, rows, body, 0, unroll=8)


def run_update(perm, mixing):
    members, rows, cols = perm.shape
    flat = perm.reshape(members * rows, cols)
    out = pl.pallas_call(
        update_kernel,
        out_shape=jax.ShapeDtypeStruct(flat.shape, jnp.float32),
        cost_estimate=pl.CostEstimate(
            flops=2 * members * members * rows * cols, transcendentals=0, bytes_accessed=8 * members * rows * cols
        ),
    )(mixing.T, flat)
    return out.reshape(perm.shape)


def blending_weights(predicted, observed, obs_var, perturb):
    member_count = predicted.shape[0]
    ensemble_spread = math.sqrt(member_count - 1)
    centred = (predicted - jnp.mean(predicted, axis=0, keepdims=True)) / ensemble_spread
    innovation = observed[None, :] + jnp.sqrt(obs_var)[None, :] * perturb - predicted
    weighted = centred / obs_var[None, :]
    system = jnp.eye(member_count, dtype=centred.dtype) + jnp.dot(
        weighted, centred.T, precision=lax.Precision.HIGHEST
    )
    right_side = jnp.dot(weighted, innovation.T, precision=lax.Precision.HIGHEST)
    factor = jnp.linalg.cholesky(system)
    half_solved = lax.linalg.triangular_solve(factor, right_side, left_side=True, lower=True)
    return lax.linalg.triangular_solve(
        factor, half_solved, left_side=True, lower=True, transpose_a=True
    )


def per_device(
    logarithmic_conductivity,
    starting_head,
    recharge,
    well_cells,
    well_owner,
    observed,
    obs_var,
    perturb,
):
    member_count, row_count, col_count = logarithmic_conductivity.shape
    width = STEPS
    ext_rows, ext_cols = row_count + 8, 2 * col_count
    f32 = jnp.float32

    def stack_rows(lo, hi):
        return jnp.concatenate(
            [logarithmic_conductivity[:, lo:hi], starting_head[:, lo:hi].astype(f32), recharge[None, lo:hi]], axis=0
        )

    top_rows = jnp.moveaxis(stack_rows(0, width), 1, 0)
    bottom_rows = jnp.moveaxis(stack_rows(row_count - width, row_count), 1, 0)
    from_above = jnp.moveaxis(send(bottom_rows, "row", True), 0, 1)
    from_below = jnp.moveaxis(send(top_rows, "row", False), 0, 1)
    stacked_total = from_above.shape[0]
    halo_rows = jnp.concatenate(
        [from_below, jnp.zeros((stacked_total, 8 - 2 * width, col_count), f32), from_above], axis=1
    )

    highest = lax.Precision.HIGHEST
    lane = jnp.arange(col_count)
    pick = jnp.arange(8)
    wanted = jnp.where(pick < width, pick, col_count - 8 + pick)
    selector = ((pick[:, None] < width) | (pick[:, None] >= 8 - width)) & (lane[None, :] == wanted[:, None])
    selector = selector.astype(f32)

    def columns(block):
        flat = block.reshape(-1, col_count)
        if block.dtype == jnp.bfloat16:
            return jnp.dot(selector.astype(jnp.bfloat16), flat.T, preferred_element_type=f32)
        return jnp.dot(selector, flat.T, precision=highest)

    interior_cols = jnp.concatenate(
        [
            columns(logarithmic_conductivity).reshape(8, member_count, row_count),
            columns(starting_head).reshape(8, member_count, row_count),
            columns(recharge).reshape(8, 1, row_count),
        ],
        axis=1,
    )
    border_cols = jnp.concatenate([interior_cols, columns(halo_rows).reshape(8, stacked_total, 8)], axis=2)
    from_left = send(border_cols[8 - width :], "col", True)
    from_right = send(border_cols[:width], "col", False)
    received = jnp.concatenate([from_right, jnp.zeros((8 - 2 * width,) + from_right.shape[1:], f32), from_left], axis=0)
    halo_cols = jnp.einsum("kmr,kl->mrl", received, selector, precision=highest)
    inside = circular_inside("row", row_count, width, ext_rows)[:, None] & circular_inside(
        "col", col_count, width, ext_cols
    )[None, :]
    pressure_low, hydraulic_head = run_stencil(
        inside.astype(f32), recharge, halo_rows, halo_cols, logarithmic_conductivity, starting_head, 8
    )
    group_total, well_count = well_cells.shape
    local_data = jnp.take(hydraulic_head.reshape(member_count, row_count * col_count), well_cells.reshape(-1), axis=1, mode="clip")
    me = lax.axis_index("row") * lax.axis_size("col") + lax.axis_index("col")
    mine = jnp.repeat(well_owner == me, well_count)
    local_data = jnp.where(mine[None, :], local_data, 0.0)
    predicted = broadcast_from_owners(local_data, ("row", "col"))
    mixing = blending_weights(predicted, observed, obs_var, perturb)
    updated_perm = run_update(logarithmic_conductivity, mixing)
    return (pressure_low, predicted, updated_perm)


def solution(mesh):
    return jax.shard_map(
        per_device,
        mesh=mesh,
        in_specs=(
            P(None, "row", "col"),
            P(None, "row", "col"),
            P("row", "col"),
            P(),
            P(),
            P(),
            P(),
            P(),
        ),
        out_specs=(P(None, "row", "col"), P(), P(None, "row", "col")),
        check_vma=False,
    )
```
